32 devices in a mesh: lat: 8 (over y, x, core), lon: 4 (over z).
Axes of the slice: x: 2, y: 2, z: 4, core: 2. Of those that a mesh axis runs over, the one named last changes fastest.
Arguments:
- surface: float32 [256, 8192], P('lat', 'lon'), may hold values from -6 to 6
- wet_blocks: int32 [256, 64], P('lat', 'lon'), may hold values 0 or 1
- legendre: float32 [1024, 256, 1024], P('lon', 'lat'), may hold values from -0.375 to 0.375
- slot_order: int32 [1024], replicated, may hold values from 0 to 1023, each once
- love_gain: float32 [1024], replicated, may hold values from 0.25 to 2.5
Outputs:
- surface_next: float32 [256, 8192], P('lat', 'lon')
- loading: float32 [256, 8192], P('lat', 'lon')
The draws below stay inside these ranges and needn't reach their ends.
Inputs may be any that keep to these rules, and one draw needn't show every extreme that they name: `slot_order`: each order 0 to 1023 is held by exactly one slot.
All inputs are finite; a program needn't handle non-finite values. No bound on the sum of `wet_blocks` on one device may be relied on, other than what follows from the above.
Results may differ from the reference program's by a relative error of at most 0.000073.
Values sent between devices are 32-bit elements; how exact they have to be, the bound alone decides.
No kernel may reach another device: no remote copies, remote signals or barrier semaphores. Data moves between devices by JAX's collectives and lax.ppermute only.
A program may use at most 192 MiB of HBM per device.

```python
import math
import jax
import jax.numpy as jnp
from jax import lax

NLON = 8192
LL = 1024
BLK = 128
CYCLES = 256


def with_ends(result, key, low, high):
    longest = result.shape.index(max(result.shape))
    spots = []
    for shift in (0, 1):
        where = [jax.random.randint(jax.random.fold_in(key, axis), (), 0, length) for axis, length in enumerate(result.shape)]
        where[longest] = (where[longest] + shift) % result.shape[longest]
        spots.append(tuple(where))
    return result.at[spots[0]].set(low).at[spots[1]].set(high)


def steps_of(own_key, extent, shards, least, largest):
    def one(axis_at, parts):
        draws = jax.random.uniform(jax.random.fold_in(jax.random.fold_in(own_key, 6), axis_at), (parts,), jnp.float32, least / len(shards), largest / len(shards))
        return jnp.repeat(jnp.exp(draws), extent[axis_at] // parts).reshape((-1,) + (1,) * (len(extent) - axis_at - 1))

    level = one(*shards[0])
    for cut in shards[1:]:
        level = level * one(*cut)
    return level


def gaussian(rng, shape, width, reach, shards=(), kind=jnp.bfloat16):
    drawn = jax.random.normal(rng, shape, jnp.float32) * width
    if len(shards) > 0:
        drawn = steps_of(rng, shape, shards, -0.22, 0.18) * drawn
    return jnp.clip(drawn, min=-reach, max=reach).astype(kind)


def setup_inputs(seed: int = 0) -> dict:
    splits = jax.random.split(jax.random.key(seed), 6)
    surface = gaussian(splits[0], (CYCLES, NLON), 1.0, 6.0, ((0, 8), (1, 4)), jnp.float32)
    wet_blocks = with_ends((jax.random.randint(splits[1], (CYCLES, NLON // BLK), 0, 4) < 3).astype(jnp.int32), jax.random.fold_in(splits[1], 1), 0, 1)
    legendre = gaussian(splits[2], (LL, CYCLES, LL), CYCLES ** -0.5, 0.375, ((0, 4), (1, 8)), jnp.float32)
    slot_order = jax.random.permutation(splits[3], LL).astype(jnp.int32)
    love_gain = jnp.clip(jnp.exp(jax.random.uniform(splits[4], (LL,), jnp.float32, math.log(0.25), math.log(2.5))), 0.25, 2.5)
    return dict(surface=surface, wet_blocks=wet_blocks, legendre=legendre, slot_order=slot_order, love_gain=love_gain)


def fourier_table(orders, positions, lon_total):
    phase = (orders[:, None] * positions[None, :]) % lon_total
    angle = phase.astype(jnp.float32) * (2.0 * math.pi / lon_total)
    return jnp.stack([jnp.cos(angle), jnp.sin(angle)], axis=1)


def reference(surface, wet_blocks, legendre, slot_order, love_gain):
    lon_total = surface.shape[1]
    wet_cells = jnp.repeat(wet_blocks, BLK, axis=1).astype(jnp.float32)
    masked = wet_cells * surface
    positions = jnp.arange(lon_total, dtype=jnp.int32)
    phases = fourier_table(slot_order, positions, lon_total)
    fourier = jnp.einsum('kcx,rx->kcr', phases, masked, precision=lax.Precision.HIGHEST) * (lon_total ** -0.5)
    coefficient = jnp.einsum('krl,kcr->kcl', legendre, fourier, precision=lax.Precision.HIGHEST)
    degrees = jnp.arange(LL, dtype=jnp.int32)
    retained = degrees[None, :] >= slot_order[:, None]
    spectrum = jnp.where(retained[:, None, :], love_gain[None, None, :] * coefficient, 0.0)
    synthesis = jnp.einsum('krl,kcl->kcr', legendre, spectrum, precision=lax.Precision.HIGHEST)
    loading = jnp.einsum('kcr,kcx->rx', synthesis, phases, precision=lax.Precision.HIGHEST) * ((2 * LL) ** -0.5)
    potential = masked - 0.6 * loading
    padded = jnp.pad(potential, 1)
    neighbours = padded[2:, 1:-1] + padded[:-2, 1:-1] + padded[1:-1, 2:] + padded[1:-1, :-2]
    surface_next = wet_cells * (masked + 0.2 * (neighbours - 4.0 * potential))
    return surface_next, loading
```

```python
import math

import jax
import jax.numpy as jnp
from jax import lax
from jax.sharding import PartitionSpec as P

BLK = 128


def padded_2(cells, sides, width):
    for axis, dim in sides:
        count = lax.axis_size(axis)
        ends = count - 1
        head = lax.slice_in_dim(cells, 0, width, axis=dim)
        tail = lax.slice_in_dim(cells, cells.shape[dim] - width, cells.shape[dim], axis=dim)
        cells = jnp.concatenate(
            [
                lax.ppermute(tail, axis, [(i, (i + 1) % count) for i in range(ends)]),
                cells,
                lax.ppermute(head, axis, [((i + 1) % count, i) for i in range(ends)]),
            ],
            axis=dim,
        )
    return cells


def fourier_table(orders, lon_start, lon_width, lon_total):
    inner_n = 64 if lon_width % 64 == 0 else lon_width
    outer_n = lon_width // inner_n
    scale = 2.0 * math.pi / lon_total

    def angle(pos):
        phase = orders[:, None] * pos[None, :] % lon_total
        return phase.astype(jnp.float32) * scale

    outer = angle(lon_start + inner_n * jnp.arange(outer_n, dtype=jnp.int32))
    inner = angle(jnp.arange(inner_n, dtype=jnp.int32))
    ca, sa = jnp.cos(outer)[:, :, None], jnp.sin(outer)[:, :, None]
    cb, sb = jnp.cos(inner)[:, None, :], jnp.sin(inner)[:, None, :]
    cos = ca * cb - sa * sb
    sin = sa * cb + ca * sb
    return jnp.stack([cos, sin], axis=1).reshape(orders.shape[0], 2, lon_width)


def reduce_scatter(x, axis):
    count = lax.axis_size(axis)
    moved = lax.all_to_all(x, axis, 0, 0, tiled=True)
    return moved.reshape((count, x.shape[0] // count) + x.shape[1:]).sum(axis=0)


def all_gather(x, axis):
    count = lax.axis_size(axis)
    copies = jnp.broadcast_to(x[None], (count,) + x.shape).reshape((count * x.shape[0],) + x.shape[1:])
    return lax.all_to_all(copies, axis, 0, 0, tiled=True)


def local(surface, wet_blocks, legendre, slot_order, love_gain):
    cycle_count, lon_width = surface.shape
    groups = lax.axis_size("lon")
    lon_total = lon_width * groups
    slot_count = legendre.shape[0]
    slot_total = slot_count * groups
    wet_cells = jnp.repeat(wet_blocks, BLK, axis=1).astype(jnp.float32)
    masked = wet_cells * surface
    lon_start = lax.axis_index("lon") * lon_width
    own_orders = lax.dynamic_slice_in_dim(
        slot_order, lax.axis_index("lon") * slot_count, slot_count
    )
    forward_scale = lon_total ** (-0.5)
    phases = fourier_table(slot_order, lon_start, lon_width, lon_total)
    fourier = reduce_scatter(
        jnp.einsum("kcx,rx->kcr", phases, masked, precision=lax.Precision.HIGHEST) * forward_scale,
        "lon",
    )
    coefficient = jnp.einsum("krl,kcr->kcl", legendre, fourier, precision=lax.Precision.HIGHEST)
    degree_whole = all_gather(reduce_scatter(coefficient, "lat"), "lat")
    degree_count = degree_whole.shape[2]
    degrees = jnp.arange(degree_count, dtype=jnp.int32)
    retained = degrees[None, :] >= own_orders[:, None]
    spectrum = jnp.where(retained[:, None, :], love_gain[None, None, :] * degree_whole, 0.0)
    synthesis = jnp.einsum("krl,kcl->kcr", legendre, spectrum, precision=lax.Precision.HIGHEST)
    summed = jnp.einsum(
        "kcr,kcx->rx",
        all_gather(synthesis, "lon"),
        phases,
        precision=lax.Precision.HIGHEST,
    )
    loading = summed * (2 * slot_total) ** (-0.5)
    potential = masked - 0.6 * loading
    padded = padded_2(potential, (("lat", 0), ("lon", 1)), 1)
    neighbours = padded[2:, 1:-1] + padded[:-2, 1:-1] + padded[1:-1, 2:] + padded[1:-1, :-2]
    surface_next = wet_cells * (masked + 0.2 * (neighbours - 4.0 * potential))
    return (surface_next, loading)


def solution(mesh):
    return jax.shard_map(
        local,
        mesh=mesh,
        in_specs=(P("lat", "lon"), P("lat", "lon"), P("lon", "lat", None), P(), P()),
        out_specs=(P("lat", "lon"), P("lat", "lon")),
        check_vma=False,
    )
```

```python
import math

import jax
import jax.numpy as jnp
from jax import lax
from jax.sharding import PartitionSpec as P

BLK = 128


def padded_2(cells, sides, width):
    for axis, dim in sides:
        count = lax.axis_size(axis)
        ends = count - 1
        head = lax.slice_in_dim(cells, 0, width, axis=dim)
        tail = lax.slice_in_dim(cells, cells.shape[dim] - width, cells.shape[dim], axis=dim)
        cells = jnp.concatenate(
            [
                lax.ppermute(tail, axis, [(i, (i + 1) % count) for i in range(ends)]),
                cells,
                lax.ppermute(head, axis, [((i + 1) % count, i) for i in range(ends)]),
            ],
            axis=dim,
        )
    return cells


INNER = 32


def dft_tables(order_count, lon_start, lon_width, lon_total):
    period = lon_total // INNER
    outer = jnp.arange(lon_width // INNER, dtype=jnp.int32)
    residue = jnp.arange(period, dtype=jnp.int32)
    alpha = (residue[:, None] * outer[None, :] % period).astype(jnp.float32) * (2.0 * math.pi / period)
    orders = jnp.arange(order_count, dtype=jnp.int32)
    inner = lon_start + jnp.arange(INNER, dtype=jnp.int32)
    beta = (orders[:, None] * inner[None, :] % lon_total).astype(jnp.float32) * (2.0 * math.pi / lon_total)
    beta = beta.reshape(order_count // period, period, INNER)
    return jnp.stack([jnp.cos(alpha), jnp.sin(alpha)]), jnp.cos(beta), jnp.sin(beta)


def forward_dft(masked, slot_order, lon_start, lon_total):
    cycles, lon_width = masked.shape
    order_count = slot_order.shape[0]
    rotor, cb, sb = dft_tables(order_count, lon_start, lon_width, lon_total)
    blocks = masked.reshape(cycles, lon_width // INNER, INNER)
    partial = jnp.einsum("cua,rab->cubr", rotor, blocks, precision=lax.Precision.HIGHEST)
    gc, gs = partial[0][None], partial[1][None]
    fc = (cb[..., None] * gc - sb[..., None] * gs).sum(axis=2)
    fs = (sb[..., None] * gc + cb[..., None] * gs).sum(axis=2)
    by_order = jnp.stack([fc, fs], axis=2).reshape(order_count, 2, cycles)
    return jnp.take(by_order, slot_order, axis=0)


def inverse_dft(synthesis, slot_order, lon_start, lon_width, lon_total):
    order_count, _, cycles = synthesis.shape
    rotor, cb, sb = dft_tables(order_count, lon_start, lon_width, lon_total)
    slot_of = jnp.zeros((order_count,), jnp.int32).at[slot_order].set(jnp.arange(order_count, dtype=jnp.int32))
    by_order = jnp.take(synthesis, slot_of, axis=0).reshape(cb.shape[0], cb.shape[1], 2, cycles)
    yc, ys = by_order[:, :, 0, None, :], by_order[:, :, 1, None, :]
    hc = (yc * cb[..., None] + ys * sb[..., None]).sum(axis=0)
    hs = (ys * cb[..., None] - yc * sb[..., None]).sum(axis=0)
    out = jnp.einsum("cua,cubr->rab", rotor, jnp.stack([hc, hs]), precision=lax.Precision.HIGHEST)
    return out.reshape(cycles, lon_width)


def reduce_scatter(x, axis):
    count = lax.axis_size(axis)
    moved = lax.all_to_all(x, axis, 0, 0, tiled=True)
    return moved.reshape((count, x.shape[0] // count) + x.shape[1:]).sum(axis=0)


def all_gather(x, axis):
    count = lax.axis_size(axis)
    copies = jnp.broadcast_to(x[None], (count,) + x.shape).reshape((count * x.shape[0],) + x.shape[1:])
    return lax.all_to_all(copies, axis, 0, 0, tiled=True)


def local(surface, wet_blocks, legendre, slot_order, love_gain):
    cycle_count, lon_width = surface.shape
    groups = lax.axis_size("lon")
    lon_total = lon_width * groups
    slot_count = legendre.shape[0]
    slot_total = slot_count * groups
    wet_cells = jnp.repeat(wet_blocks, BLK, axis=1).astype(jnp.float32)
    masked = wet_cells * surface
    lon_start = lax.axis_index("lon") * lon_width
    own_orders = lax.dynamic_slice_in_dim(
        slot_order, lax.axis_index("lon") * slot_count, slot_count
    )
    forward_scale = lon_total ** (-0.5)
    fourier = reduce_scatter(forward_dft(masked, slot_order, lon_start, lon_total) * forward_scale, "lon")
    coefficient = jnp.einsum("krl,kcr->kcl", legendre, fourier, precision=lax.Precision.HIGHEST)
    degree_whole = all_gather(reduce_scatter(coefficient, "lat"), "lat")
    degree_count = degree_whole.shape[2]
    degrees = jnp.arange(degree_count, dtype=jnp.int32)
    retained = degrees[None, :] >= own_orders[:, None]
    spectrum = jnp.where(retained[:, None, :], love_gain[None, None, :] * degree_whole, 0.0)
    synthesis = jnp.einsum("krl,kcl->kcr", legendre, spectrum, precision=lax.Precision.HIGHEST)
    summed = inverse_dft(all_gather(synthesis, "lon"), slot_order, lon_start, lon_width, lon_total)
    loading = summed * (2 * slot_total) ** (-0.5)
    potential = masked - 0.6 * loading
    padded = padded_2(potential, (("lat", 0), ("lon", 1)), 1)
    neighbours = padded[2:, 1:-1] + padded[:-2, 1:-1] + padded[1:-1, 2:] + padded[1:-1, :-2]
    surface_next = wet_cells * (masked + 0.2 * (neighbours - 4.0 * potential))
    return (surface_next, loading)


def solution(mesh):
    return jax.shard_map(
        local,
        mesh=mesh,
        in_specs=(P("lat", "lon"), P("lat", "lon"), P("lon", "lat", None), P(), P()),
        out_specs=(P("lat", "lon"), P("lat", "lon")),
        check_vma=False,
    )
```

```python
import math

import jax
import jax.numpy as jnp
from jax import lax
from jax.sharding import PartitionSpec as P

BLK = 128


def padded_2(cells, sides, width):
    for axis, dim in sides:
        count = lax.axis_size(axis)
        ends = count - 1
        head = lax.slice_in_dim(cells, 0, width, axis=dim)
        tail = lax.slice_in_dim(cells, cells.shape[dim] - width, cells.shape[dim], axis=dim)
        cells = jnp.concatenate(
            [
                lax.ppermute(tail, axis, [(i, (i + 1) % count) for i in range(ends)]),
                cells,
                lax.ppermute(head, axis, [((i + 1) % count, i) for i in range(ends)]),
            ],
            axis=dim,
        )
    return cells


INNER = 32


def dft_tables(order_count, lon_start, lon_width, lon_total):
    period = lon_total // INNER
    outer = jnp.arange(lon_width // INNER, dtype=jnp.int32)
    residue = jnp.arange(period, dtype=jnp.int32)
    alpha = (residue[:, None] * outer[None, :] % period).astype(jnp.float32) * (2.0 * math.pi / period)
    orders = jnp.arange(order_count, dtype=jnp.int32)
    inner = lon_start + jnp.arange(INNER, dtype=jnp.int32)
    beta = (orders[:, None] * inner[None, :] % lon_total).astype(jnp.float32) * (2.0 * math.pi / lon_total)
    beta = beta.reshape(order_count // period, period, INNER)
    return jnp.stack([jnp.cos(alpha), jnp.sin(alpha)]), jnp.cos(beta), jnp.sin(beta)


def forward_dft(masked, slot_order, lon_start, lon_total):
    cycles, lon_width = masked.shape
    order_count = slot_order.shape[0]
    rotor, cb, sb = dft_tables(order_count, lon_start, lon_width, lon_total)
    blocks = masked.reshape(cycles, lon_width // INNER, INNER)
    partial = jnp.einsum("cua,rab->cubr", rotor, blocks, precision=lax.Precision.HIGHEST)
    gc, gs = partial[0][None], partial[1][None]
    fc = (cb[..., None] * gc - sb[..., None] * gs).sum(axis=2)
    fs = (sb[..., None] * gc + cb[..., None] * gs).sum(axis=2)
    by_order = jnp.stack([fc, fs], axis=2).reshape(order_count, 2, cycles)
    return jnp.take(by_order, slot_order, axis=0)


def inverse_dft(synthesis, slot_order, lon_start, lon_width, lon_total):
    order_count, _, cycles = synthesis.shape
    rotor, cb, sb = dft_tables(order_count, lon_start, lon_width, lon_total)
    slot_of = jnp.zeros((order_count,), jnp.int32).at[slot_order].set(jnp.arange(order_count, dtype=jnp.int32))
    by_order = jnp.take(synthesis, slot_of, axis=0).reshape(cb.shape[0], cb.shape[1], 2, cycles)
    yc, ys = by_order[:, :, 0, None, :], by_order[:, :, 1, None, :]
    hc = (yc * cb[..., None] + ys * sb[..., None]).sum(axis=0)
    hs = (ys * cb[..., None] - yc * sb[..., None]).sum(axis=0)
    out = jnp.einsum("cua,cubr->rab", rotor, jnp.stack([hc, hs]), precision=lax.Precision.HIGHEST)
    return out.reshape(cycles, lon_width)


def reduce_scatter(x, axis):
    count = lax.axis_size(axis)
    moved = lax.all_to_all(x, axis, 0, 0, tiled=True)
    return moved.reshape((count, x.shape[0] // count) + x.shape[1:]).sum(axis=0)


def all_gather(x, axis):
    count = lax.axis_size(axis)
    copies = jnp.broadcast_to(x[None], (count,) + x.shape).reshape((count * x.shape[0],) + x.shape[1:])
    return lax.all_to_all(copies, axis, 0, 0, tiled=True)


def local(surface, wet_blocks, legendre, slot_order, love_gain):
    cycle_count, lon_width = surface.shape
    groups = lax.axis_size("lon")
    lon_total = lon_width * groups
    slot_count = legendre.shape[0]
    slot_total = slot_count * groups
    wet_cells = jnp.repeat(wet_blocks, BLK, axis=1).astype(jnp.float32)
    masked = wet_cells * surface
    lon_start = lax.axis_index("lon") * lon_width
    own_orders = lax.dynamic_slice_in_dim(
        slot_order, lax.axis_index("lon") * slot_count, slot_count
    )
    forward_scale = lon_total ** (-0.5)
    fourier = reduce_scatter(forward_dft(masked, slot_order, lon_start, lon_total) * forward_scale, "lon")
    coefficient = jnp.einsum("krl,kcr->kcl", legendre, fourier, precision=lax.Precision.HIGH)
    degree_whole = all_gather(reduce_scatter(coefficient, "lat"), "lat")
    degree_count = degree_whole.shape[2]
    degrees = jnp.arange(degree_count, dtype=jnp.int32)
    retained = degrees[None, :] >= own_orders[:, None]
    spectrum = jnp.where(retained[:, None, :], love_gain[None, None, :] * degree_whole, 0.0)
    synthesis = jnp.einsum("krl,kcl->kcr", legendre, spectrum, precision=lax.Precision.HIGH)
    summed = inverse_dft(all_gather(synthesis, "lon"), slot_order, lon_start, lon_width, lon_total)
    loading = summed * (2 * slot_total) ** (-0.5)
    potential = masked - 0.6 * loading
    padded = padded_2(potential, (("lat", 0), ("lon", 1)), 1)
    neighbours = padded[2:, 1:-1] + padded[:-2, 1:-1] + padded[1:-1, 2:] + padded[1:-1, :-2]
    surface_next = wet_cells * (masked + 0.2 * (neighbours - 4.0 * potential))
    return (surface_next, loading)


def solution(mesh):
    return jax.shard_map(
        local,
        mesh=mesh,
        in_specs=(P("lat", "lon"), P("lat", "lon"), P("lon", "lat", None), P(), P()),
        out_specs=(P("lat", "lon"), P("lat", "lon")),
        check_vma=False,
    )
```

```python
import math

import jax
import jax.numpy as jnp
from jax import lax
from jax.sharding import PartitionSpec as P

BLK = 128


def padded_2(cells, sides, width):
    for axis, dim in sides:
        count = lax.axis_size(axis)
        ends = count - 1
        head = lax.slice_in_dim(cells, 0, width, axis=dim)
        tail = lax.slice_in_dim(cells, cells.shape[dim] - width, cells.shape[dim], axis=dim)
        cells = jnp.concatenate(
            [
                lax.ppermute(tail, axis, [(i, (i + 1) % count) for i in range(ends)]),
                cells,
                lax.ppermute(head, axis, [((i + 1) % count, i) for i in range(ends)]),
            ],
            axis=dim,
        )
    return cells


INNER = 32


def dft_tables(order_count, lon_start, lon_width, lon_total):
    period = lon_total // INNER
    outer = jnp.arange(lon_width // INNER, dtype=jnp.int32)
    residue = jnp.arange(period, dtype=jnp.int32)
    alpha = (residue[:, None] * outer[None, :] % period).astype(jnp.float32) * (2.0 * math.pi / period)
    orders = jnp.arange(order_count, dtype=jnp.int32)
    inner = lon_start + jnp.arange(INNER, dtype=jnp.int32)
    beta = (orders[:, None] * inner[None, :] % lon_total).astype(jnp.float32) * (2.0 * math.pi / lon_total)
    beta = beta.reshape(order_count // period, period, INNER)
    return jnp.stack([jnp.cos(alpha), jnp.sin(alpha)]), jnp.cos(beta), jnp.sin(beta)


def forward_dft(masked, slot_order, lon_start, lon_total):
    cycles, lon_width = masked.shape
    order_count = slot_order.shape[0]
    rotor, cb, sb = dft_tables(order_count, lon_start, lon_width, lon_total)
    blocks = masked.reshape(cycles, lon_width // INNER, INNER)
    partial = jnp.einsum("cua,rab->cubr", rotor, blocks, precision=lax.Precision.HIGHEST)
    gc, gs = partial[0][None], partial[1][None]
    fc = (cb[..., None] * gc - sb[..., None] * gs).sum(axis=2)
    fs = (sb[..., None] * gc + cb[..., None] * gs).sum(axis=2)
    by_order = jnp.stack([fc, fs], axis=2).reshape(order_count, 2, cycles)
    return jnp.take(by_order, slot_order, axis=0)


def inverse_dft(synthesis, slot_order, lon_start, lon_width, lon_total):
    order_count, _, cycles = synthesis.shape
    rotor, cb, sb = dft_tables(order_count, lon_start, lon_width, lon_total)
    slot_of = jnp.zeros((order_count,), jnp.int32).at[slot_order].set(jnp.arange(order_count, dtype=jnp.int32))
    by_order = jnp.take(synthesis, slot_of, axis=0).reshape(cb.shape[0], cb.shape[1], 2, cycles)
    yc, ys = by_order[:, :, 0, None, :], by_order[:, :, 1, None, :]
    hc = (yc * cb[..., None] + ys * sb[..., None]).sum(axis=0)
    hs = (ys * cb[..., None] - yc * sb[..., None]).sum(axis=0)
    out = jnp.einsum("cua,cubr->rab", rotor, jnp.stack([hc, hs]), precision=lax.Precision.HIGHEST)
    return out.reshape(cycles, lon_width)


def reduce_scatter(x, axis):
    count = lax.axis_size(axis)
    moved = lax.all_to_all(x, axis, 0, 0, tiled=True)
    return moved.reshape((count, x.shape[0] // count) + x.shape[1:]).sum(axis=0)


def all_gather(x, axis):
    count = lax.axis_size(axis)
    copies = jnp.broadcast_to(x[None], (count,) + x.shape).reshape((count * x.shape[0],) + x.shape[1:])
    return lax.all_to_all(copies, axis, 0, 0, tiled=True)


def paired_reduce_scatter(x, axis):
    count = lax.axis_size(axis)
    pairs = [(i, i ^ 1) for i in range(count)]
    groups = [list(range(side, count, 2)) for side in (0, 1)]
    side = lax.axis_index(axis) % 2
    half = x.shape[0] // 2
    kept = lax.dynamic_slice_in_dim(x, side * half, half)
    sent = lax.dynamic_slice_in_dim(x, (1 - side) * half, half)
    summed = kept + lax.ppermute(sent, axis, pairs)
    moved = lax.all_to_all(summed, axis, 0, 0, tiled=True, axis_index_groups=groups)
    return moved.reshape((count // 2, half * 2 // count) + x.shape[1:]).sum(axis=0)


def paired_all_gather(x, axis):
    count = lax.axis_size(axis)
    pairs = [(i, i ^ 1) for i in range(count)]
    groups = [list(range(side, count, 2)) for side in (0, 1)]
    side = lax.axis_index(axis) % 2
    copies = jnp.broadcast_to(x[None], (count // 2,) + x.shape).reshape((count // 2 * x.shape[0],) + x.shape[1:])
    half = lax.all_to_all(copies, axis, 0, 0, tiled=True, axis_index_groups=groups)
    other = lax.ppermute(half, axis, pairs)
    return jnp.where(side == 0, jnp.concatenate([half, other]), jnp.concatenate([other, half]))


def local(surface, wet_blocks, legendre, slot_order, love_gain):
    cycle_count, lon_width = surface.shape
    groups = lax.axis_size("lon")
    lon_total = lon_width * groups
    slot_count = legendre.shape[0]
    slot_total = slot_count * groups
    wet_cells = jnp.repeat(wet_blocks, BLK, axis=1).astype(jnp.float32)
    masked = wet_cells * surface
    lon_start = lax.axis_index("lon") * lon_width
    own_orders = lax.dynamic_slice_in_dim(
        slot_order, lax.axis_index("lon") * slot_count, slot_count
    )
    forward_scale = lon_total ** (-0.5)
    fourier = reduce_scatter(forward_dft(masked, slot_order, lon_start, lon_total) * forward_scale, "lon")
    coefficient = jnp.einsum("krl,kcr->kcl", legendre, fourier, precision=lax.Precision.HIGH)
    degree_whole = paired_all_gather(paired_reduce_scatter(coefficient, "lat"), "lat")
    degree_count = degree_whole.shape[2]
    degrees = jnp.arange(degree_count, dtype=jnp.int32)
    retained = degrees[None, :] >= own_orders[:, None]
    spectrum = jnp.where(retained[:, None, :], love_gain[None, None, :] * degree_whole, 0.0)
    synthesis = jnp.einsum("krl,kcl->kcr", legendre, spectrum, precision=lax.Precision.HIGH)
    summed = inverse_dft(all_gather(synthesis, "lon"), slot_order, lon_start, lon_width, lon_total)
    loading = summed * (2 * slot_total) ** (-0.5)
    potential = masked - 0.6 * loading
    padded = padded_2(potential, (("lat", 0), ("lon", 1)), 1)
    neighbours = padded[2:, 1:-1] + padded[:-2, 1:-1] + padded[1:-1, 2:] + padded[1:-1, :-2]
    surface_next = wet_cells * (masked + 0.2 * (neighbours - 4.0 * potential))
    return (surface_next, loading)


def solution(mesh):
    return jax.shard_map(
        local,
        mesh=mesh,
        in_specs=(P("lat", "lon"), P("lat", "lon"), P("lon", "lat", None), P(), P()),
        out_specs=(P("lat", "lon"), P("lat", "lon")),
        check_vma=False,
    )
```

```python
import math

import jax
import jax.numpy as jnp
from jax import lax
from jax.sharding import PartitionSpec as P

BLK = 128


def halo(cells, axis, dim):
    count = lax.axis_size(axis)
    ends = count - 1
    head = lax.slice_in_dim(cells, 0, 1, axis=dim)
    tail = lax.slice_in_dim(cells, cells.shape[dim] - 1, cells.shape[dim], axis=dim)
    before = lax.ppermute(tail, axis, [(i, (i + 1) % count) for i in range(ends)])
    after = lax.ppermute(head, axis, [((i + 1) % count, i) for i in range(ends)])
    return before, after


def neighbour_sum(cells):
    up, down = halo(cells, "lat", 0)
    left, right = halo(cells, "lon", 1)
    rows = jnp.concatenate([up, cells[:-1]], axis=0) + jnp.concatenate([cells[1:], down], axis=0)
    cols = jnp.concatenate([left, cells[:, :-1]], axis=1) + jnp.concatenate([cells[:, 1:], right], axis=1)
    return rows + cols


INNER = 32


def dft_tables(order_count, lon_start, lon_width, lon_total):
    period = lon_total // INNER
    outer = jnp.arange(lon_width // INNER, dtype=jnp.int32)
    residue = jnp.arange(period, dtype=jnp.int32)
    alpha = (residue[:, None] * outer[None, :] % period).astype(jnp.float32) * (2.0 * math.pi / period)
    orders = jnp.arange(order_count, dtype=jnp.int32)
    inner = lon_start + jnp.arange(INNER, dtype=jnp.int32)
    beta = (orders[:, None] * inner[None, :] % lon_total).astype(jnp.float32) * (2.0 * math.pi / lon_total)
    beta = beta.reshape(order_count // period, period, INNER)
    return jnp.stack([jnp.cos(alpha), jnp.sin(alpha)]), jnp.cos(beta), jnp.sin(beta)


def forward_dft(masked, slot_order, lon_start, lon_total):
    cycles, lon_width = masked.shape
    order_count = slot_order.shape[0]
    rotor, cb, sb = dft_tables(order_count, lon_start, lon_width, lon_total)
    blocks = masked.reshape(cycles, lon_width // INNER, INNER)
    partial = jnp.einsum("cua,rab->cubr", rotor, blocks, precision=lax.Precision.HIGHEST)
    gc, gs = partial[0][None], partial[1][None]
    fc = (cb[..., None] * gc - sb[..., None] * gs).sum(axis=2)
    fs = (sb[..., None] * gc + cb[..., None] * gs).sum(axis=2)
    by_order = jnp.stack([fc, fs], axis=2).reshape(order_count, 2, cycles)
    return jnp.take(by_order, slot_order, axis=0)


def inverse_dft(synthesis, slot_order, lon_start, lon_width, lon_total):
    order_count, _, cycles = synthesis.shape
    rotor, cb, sb = dft_tables(order_count, lon_start, lon_width, lon_total)
    slots = jnp.arange(order_count, dtype=jnp.int32)
    slot_of = jnp.where(slot_order[None, :] == slots[:, None], slots[None, :], 0).sum(axis=1)
    by_order = jnp.take(synthesis, slot_of, axis=0).reshape(cb.shape[0], cb.shape[1], 2, cycles)
    yc, ys = by_order[:, :, 0, None, :], by_order[:, :, 1, None, :]
    hc = (yc * cb[..., None] + ys * sb[..., None]).sum(axis=0)
    hs = (ys * cb[..., None] - yc * sb[..., None]).sum(axis=0)
    out = jnp.einsum("cua,cubr->rab", rotor, jnp.stack([hc, hs]), precision=lax.Precision.HIGHEST)
    return out.reshape(cycles, lon_width)


def shifted_reduce_scatter(x, axis):
    count = lax.axis_size(axis)
    me = lax.axis_index(axis)
    size = x.shape[0] // count
    total = lax.dynamic_slice_in_dim(x, me * size, size)
    for shift in range(1, count):
        chunk = lax.dynamic_slice_in_dim(x, (me + shift) % count * size, size)
        total = total + lax.ppermute(chunk, axis, [(i, (i + shift) % count) for i in range(count)])
    return total


def shifted_all_gather(x, axis):
    count = lax.axis_size(axis)
    me = lax.axis_index(axis)
    ahead = [x] + [lax.ppermute(x, axis, [((i + shift) % count, i) for i in range(count)]) for shift in range(1, count)]
    stacked = jnp.concatenate(ahead + ahead, axis=0)
    return lax.dynamic_slice_in_dim(stacked, (count - me) % count * x.shape[0], count * x.shape[0])


def paired_reduce_scatter(x, axis):
    count = lax.axis_size(axis)
    pairs = [(i, i ^ 1) for i in range(count)]
    groups = [list(range(side, count, 2)) for side in (0, 1)]
    side = lax.axis_index(axis) % 2
    half = x.shape[0] // 2
    kept = lax.dynamic_slice_in_dim(x, side * half, half)
    sent = lax.dynamic_slice_in_dim(x, (1 - side) * half, half)
    summed = kept + lax.ppermute(sent, axis, pairs)
    moved = lax.all_to_all(summed, axis, 0, 0, tiled=True, axis_index_groups=groups)
    return moved.reshape((count // 2, half * 2 // count) + x.shape[1:]).sum(axis=0)


def paired_all_gather(x, axis):
    count = lax.axis_size(axis)
    pairs = [(i, i ^ 1) for i in range(count)]
    groups = [list(range(side, count, 2)) for side in (0, 1)]
    side = lax.axis_index(axis) % 2
    copies = jnp.broadcast_to(x[None], (count // 2,) + x.shape).reshape((count // 2 * x.shape[0],) + x.shape[1:])
    half = lax.all_to_all(copies, axis, 0, 0, tiled=True, axis_index_groups=groups)
    other = lax.ppermute(half, axis, pairs)
    return jnp.where(side == 0, jnp.concatenate([half, other]), jnp.concatenate([other, half]))


def local(surface, wet_blocks, legendre, slot_order, love_gain):
    cycle_count, lon_width = surface.shape
    groups = lax.axis_size("lon")
    lon_total = lon_width * groups
    slot_count = legendre.shape[0]
    slot_total = slot_count * groups
    wet_cells = jnp.repeat(wet_blocks, BLK, axis=1).astype(jnp.float32)
    masked = wet_cells * surface
    lon_start = lax.axis_index("lon") * lon_width
    own_orders = lax.dynamic_slice_in_dim(
        slot_order, lax.axis_index("lon") * slot_count, slot_count
    )
    forward_scale = lon_total ** (-0.5)
    fourier = shifted_reduce_scatter(forward_dft(masked, slot_order, lon_start, lon_total) * forward_scale, "lon")
    coefficient = jnp.einsum("krl,kcr->kcl", legendre, fourier, precision=lax.Precision.HIGH)
    degree_whole = paired_all_gather(paired_reduce_scatter(coefficient, "lat"), "lat")
    degree_count = degree_whole.shape[2]
    degrees = jnp.arange(degree_count, dtype=jnp.int32)
    retained = degrees[None, :] >= own_orders[:, None]
    spectrum = jnp.where(retained[:, None, :], love_gain[None, None, :] * degree_whole, 0.0)
    synthesis = jnp.einsum("krl,kcl->kcr", legendre, spectrum, precision=lax.Precision.HIGH)
    summed = inverse_dft(shifted_all_gather(synthesis, "lon"), slot_order, lon_start, lon_width, lon_total)
    loading = summed * (2 * slot_total) ** (-0.5)
    potential = masked - 0.6 * loading
    neighbours = neighbour_sum(potential)
    surface_next = wet_cells * (masked + 0.2 * (neighbours - 4.0 * potential))
    return (surface_next, loading)


def solution(mesh):
    return jax.shard_map(
        local,
        mesh=mesh,
        in_specs=(P("lat", "lon"), P("lat", "lon"), P("lon", "lat", None), P(), P()),
        out_specs=(P("lat", "lon"), P("lat", "lon")),
        check_vma=False,
    )
```

```python
import math

import jax
import jax.numpy as jnp
from jax import lax
from jax.sharding import PartitionSpec as P

BLK = 128


def halo(cells, axis, dim):
    count = lax.axis_size(axis)
    ends = count - 1
    head = lax.slice_in_dim(cells, 0, 1, axis=dim)
    tail = lax.slice_in_dim(cells, cells.shape[dim] - 1, cells.shape[dim], axis=dim)
    before = lax.ppermute(tail, axis, [(i, (i + 1) % count) for i in range(ends)])
    after = lax.ppermute(head, axis, [((i + 1) % count, i) for i in range(ends)])
    return before, after


def neighbour_sum(cells):
    up, down = halo(cells, "lat", 0)
    left, right = halo(cells, "lon", 1)
    rows = jnp.concatenate([up, cells[:-1]], axis=0) + jnp.concatenate([cells[1:], down], axis=0)
    cols = jnp.concatenate([left, cells[:, :-1]], axis=1) + jnp.concatenate([cells[:, 1:], right], axis=1)
    return rows + cols


INNER = 32


def dft_tables(order_count, lon_start, lon_width, lon_total):
    period = lon_total // INNER
    outer = jnp.arange(lon_width // INNER, dtype=jnp.int32)
    residue = jnp.arange(period, dtype=jnp.int32)
    alpha = (residue[:, None] * outer[None, :] % period).astype(jnp.float32) * (2.0 * math.pi / period)
    orders = jnp.arange(order_count, dtype=jnp.int32)
    inner = lon_start + jnp.arange(INNER, dtype=jnp.int32)
    beta = (orders[:, None] * inner[None, :] % lon_total).astype(jnp.float32) * (2.0 * math.pi / lon_total)
    beta = beta.reshape(order_count // period, period, INNER)
    return jnp.stack([jnp.cos(alpha), jnp.sin(alpha)]), jnp.cos(beta), jnp.sin(beta)


def forward_dft(masked, slot_order, lon_start, lon_total):
    cycles, lon_width = masked.shape
    order_count = slot_order.shape[0]
    rotor, cb, sb = dft_tables(order_count, lon_start, lon_width, lon_total)
    blocks = masked.reshape(cycles, lon_width // INNER, INNER)
    partial = jnp.einsum("cua,rab->cubr", rotor, blocks, precision=lax.Precision.HIGHEST)
    gc, gs = partial[0][None], partial[1][None]
    fc = (cb[..., None] * gc - sb[..., None] * gs).sum(axis=2)
    fs = (sb[..., None] * gc + cb[..., None] * gs).sum(axis=2)
    by_order = jnp.stack([fc, fs], axis=2).reshape(order_count, 2, cycles)
    return jnp.take(by_order, slot_order, axis=0)


def inverse_dft(synthesis, slot_order, lon_start, lon_width, lon_total):
    order_count, _, cycles = synthesis.shape
    rotor, cb, sb = dft_tables(order_count, lon_start, lon_width, lon_total)
    slots = jnp.arange(order_count, dtype=jnp.int32)
    slot_of = jnp.where(slot_order[None, :] == slots[:, None], slots[None, :], 0).sum(axis=1)
    by_order = jnp.take(synthesis, slot_of, axis=0).reshape(cb.shape[0], cb.shape[1], 2, cycles)
    yc, ys = by_order[:, :, 0, None, :], by_order[:, :, 1, None, :]
    hc = (yc * cb[..., None] + ys * sb[..., None]).sum(axis=0)
    hs = (ys * cb[..., None] - yc * sb[..., None]).sum(axis=0)
    out = jnp.einsum("cua,cubr->rab", rotor, jnp.stack([hc, hs]), precision=lax.Precision.HIGHEST)
    return out.reshape(cycles, lon_width)


def reduce_scatter(x, axis):
    count = lax.axis_size(axis)
    moved = lax.all_to_all(x, axis, 0, 0, tiled=True)
    return moved.reshape((count, x.shape[0] // count) + x.shape[1:]).sum(axis=0)


def all_gather(x, axis):
    count = lax.axis_size(axis)
    copies = jnp.broadcast_to(x[None], (count,) + x.shape).reshape((count * x.shape[0],) + x.shape[1:])
    return lax.all_to_all(copies, axis, 0, 0, tiled=True)


def paired_reduce_scatter(x, axis):
    count = lax.axis_size(axis)
    pairs = [(i, i ^ 1) for i in range(count)]
    groups = [list(range(side, count, 2)) for side in (0, 1)]
    side = lax.axis_index(axis) % 2
    half = x.shape[0] // 2
    kept = lax.dynamic_slice_in_dim(x, side * half, half)
    sent = lax.dynamic_slice_in_dim(x, (1 - side) * half, half)
    summed = kept + lax.ppermute(sent, axis, pairs)
    moved = lax.all_to_all(summed, axis, 0, 0, tiled=True, axis_index_groups=groups)
    return moved.reshape((count // 2, half * 2 // count) + x.shape[1:]).sum(axis=0)


def paired_all_gather(x, axis):
    count = lax.axis_size(axis)
    pairs = [(i, i ^ 1) for i in range(count)]
    groups = [list(range(side, count, 2)) for side in (0, 1)]
    side = lax.axis_index(axis) % 2
    copies = jnp.broadcast_to(x[None], (count // 2,) + x.shape).reshape((count // 2 * x.shape[0],) + x.shape[1:])
    half = lax.all_to_all(copies, axis, 0, 0, tiled=True, axis_index_groups=groups)
    other = lax.ppermute(half, axis, pairs)
    return jnp.where(side == 0, jnp.concatenate([half, other]), jnp.concatenate([other, half]))


def local(surface, wet_blocks, legendre, slot_order, love_gain):
    cycle_count, lon_width = surface.shape
    groups = lax.axis_size("lon")
    lon_total = lon_width * groups
    slot_count = legendre.shape[0]
    slot_total = slot_count * groups
    wet_cells = jnp.repeat(wet_blocks, BLK, axis=1).astype(jnp.float32)
    masked = wet_cells * surface
    lon_start = lax.axis_index("lon") * lon_width
    own_orders = lax.dynamic_slice_in_dim(
        slot_order, lax.axis_index("lon") * slot_count, slot_count
    )
    forward_scale = lon_total ** (-0.5)
    fourier = reduce_scatter(forward_dft(masked, slot_order, lon_start, lon_total) * forward_scale, "lon")
    coefficient = jnp.einsum("krl,kcr->kcl", legendre, fourier, precision=lax.Precision.HIGH)
    degree_whole = paired_all_gather(paired_reduce_scatter(coefficient, "lat"), "lat")
    degree_count = degree_whole.shape[2]
    degrees = jnp.arange(degree_count, dtype=jnp.int32)
    retained = degrees[None, :] >= own_orders[:, None]
    spectrum = jnp.where(retained[:, None, :], love_gain[None, None, :] * degree_whole, 0.0)
    synthesis = jnp.einsum("krl,kcl->kcr", legendre, spectrum, precision=lax.Precision.HIGH)
    summed = inverse_dft(all_gather(synthesis, "lon"), slot_order, lon_start, lon_width, lon_total)
    loading = summed * (2 * slot_total) ** (-0.5)
    potential = masked - 0.6 * loading
    neighbours = neighbour_sum(potential)
    surface_next = wet_cells * (masked + 0.2 * (neighbours - 4.0 * potential))
    return (surface_next, loading)


def solution(mesh):
    return jax.shard_map(
        local,
        mesh=mesh,
        in_specs=(P("lat", "lon"), P("lat", "lon"), P("lon", "lat", None), P(), P()),
        out_specs=(P("lat", "lon"), P("lat", "lon")),
        check_vma=False,
    )
```

```python
import math

import jax
import jax.numpy as jnp
from jax import lax
from jax.sharding import PartitionSpec as P

BLK = 128


def halo(cells, axis, dim):
    count = lax.axis_size(axis)
    ends = count - 1
    head = lax.slice_in_dim(cells, 0, 1, axis=dim)
    tail = lax.slice_in_dim(cells, cells.shape[dim] - 1, cells.shape[dim], axis=dim)
    before = lax.ppermute(tail, axis, [(i, (i + 1) % count) for i in range(ends)])
    after = lax.ppermute(head, axis, [((i + 1) % count, i) for i in range(ends)])
    return before, after


def neighbour_sum(cells):
    up, down = halo(cells, "lat", 0)
    left, right = halo(cells, "lon", 1)
    rows = jnp.concatenate([up, cells[:-1]], axis=0) + jnp.concatenate([cells[1:], down], axis=0)
    cols = jnp.concatenate([left, cells[:, :-1]], axis=1) + jnp.concatenate([cells[:, 1:], right], axis=1)
    return rows + cols


INNER = 32


def dft_tables(order_count, lon_start, lon_width, lon_total):
    period = lon_total // INNER
    outer = jnp.arange(lon_width // INNER, dtype=jnp.int32)
    residue = jnp.arange(period, dtype=jnp.int32)
    alpha = (residue[:, None] * outer[None, :] % period).astype(jnp.float32) * (2.0 * math.pi / period)
    orders = jnp.arange(order_count, dtype=jnp.int32)
    inner = lon_start + jnp.arange(INNER, dtype=jnp.int32)
    beta = (orders[:, None] * inner[None, :] % lon_total).astype(jnp.float32) * (2.0 * math.pi / lon_total)
    beta = beta.reshape(order_count // period, period, INNER)
    return jnp.stack([jnp.cos(alpha), jnp.sin(alpha)]), jnp.cos(beta), jnp.sin(beta)


def forward_dft(masked, slot_order, lon_start, lon_total):
    cycles, lon_width = masked.shape
    order_count = slot_order.shape[0]
    rotor, cb, sb = dft_tables(order_count, lon_start, lon_width, lon_total)
    blocks = masked.reshape(cycles, lon_width // INNER, INNER)
    partial = jnp.einsum("cua,rab->cubr", rotor, blocks, precision=lax.Precision.HIGHEST)
    gc, gs = partial[0][None], partial[1][None]
    fc = (cb[..., None] * gc - sb[..., None] * gs).sum(axis=2)
    fs = (sb[..., None] * gc + cb[..., None] * gs).sum(axis=2)
    by_order = jnp.stack([fc, fs], axis=2).reshape(order_count, 2, cycles)
    return jnp.take(by_order, slot_order, axis=0, mode="clip", unique_indices=True)


def inverse_dft(synthesis, slot_order, lon_start, lon_width, lon_total):
    order_count, _, cycles = synthesis.shape
    rotor, cb, sb = dft_tables(order_count, lon_start, lon_width, lon_total)
    slots = jnp.arange(order_count, dtype=jnp.int32)
    slot_of = jnp.where(slot_order[None, :] == slots[:, None], slots[None, :], 0).sum(axis=1)
    by_order = jnp.take(synthesis, slot_of, axis=0, mode="clip", unique_indices=True).reshape(cb.shape[0], cb.shape[1], 2, cycles)
    yc, ys = by_order[:, :, 0, None, :], by_order[:, :, 1, None, :]
    hc = (yc * cb[..., None] + ys * sb[..., None]).sum(axis=0)
    hs = (ys * cb[..., None] - yc * sb[..., None]).sum(axis=0)
    out = jnp.einsum("cua,cubr->rab", rotor, jnp.stack([hc, hs]), precision=lax.Precision.HIGHEST)
    return out.reshape(cycles, lon_width)


def reduce_scatter(x, axis):
    count = lax.axis_size(axis)
    moved = lax.all_to_all(x, axis, 0, 0, tiled=True)
    return moved.reshape((count, x.shape[0] // count) + x.shape[1:]).sum(axis=0)


def all_gather(x, axis):
    count = lax.axis_size(axis)
    copies = jnp.broadcast_to(x[None], (count,) + x.shape).reshape((count * x.shape[0],) + x.shape[1:])
    return lax.all_to_all(copies, axis, 0, 0, tiled=True)


def paired_reduce_scatter(x, axis):
    count = lax.axis_size(axis)
    pairs = [(i, i ^ 1) for i in range(count)]
    groups = [list(range(side, count, 2)) for side in (0, 1)]
    side = lax.axis_index(axis) % 2
    half = x.shape[0] // 2
    kept = lax.dynamic_slice_in_dim(x, side * half, half)
    sent = lax.dynamic_slice_in_dim(x, (1 - side) * half, half)
    summed = kept + lax.ppermute(sent, axis, pairs)
    moved = lax.all_to_all(summed, axis, 0, 0, tiled=True, axis_index_groups=groups)
    return moved.reshape((count // 2, half * 2 // count) + x.shape[1:]).sum(axis=0)


def paired_all_gather(x, axis):
    count = lax.axis_size(axis)
    pairs = [(i, i ^ 1) for i in range(count)]
    groups = [list(range(side, count, 2)) for side in (0, 1)]
    side = lax.axis_index(axis) % 2
    copies = jnp.broadcast_to(x[None], (count // 2,) + x.shape).reshape((count // 2 * x.shape[0],) + x.shape[1:])
    half = lax.all_to_all(copies, axis, 0, 0, tiled=True, axis_index_groups=groups)
    other = lax.ppermute(half, axis, pairs)
    return jnp.where(side == 0, jnp.concatenate([half, other]), jnp.concatenate([other, half]))


def local(surface, wet_blocks, legendre, slot_order, love_gain):
    cycle_count, lon_width = surface.shape
    groups = lax.axis_size("lon")
    lon_total = lon_width * groups
    slot_count = legendre.shape[0]
    slot_total = slot_count * groups
    wet_cells = jnp.repeat(wet_blocks, BLK, axis=1).astype(jnp.float32)
    masked = wet_cells * surface
    lon_start = lax.axis_index("lon") * lon_width
    own_orders = lax.dynamic_slice_in_dim(
        slot_order, lax.axis_index("lon") * slot_count, slot_count
    )
    forward_scale = lon_total ** (-0.5)
    fourier = reduce_scatter(forward_dft(masked, slot_order, lon_start, lon_total) * forward_scale, "lon")
    coefficient = jnp.einsum("krl,kcr->kcl", legendre, fourier, precision=lax.Precision.HIGH)
    degree_whole = paired_all_gather(paired_reduce_scatter(coefficient, "lat"), "lat")
    degree_count = degree_whole.shape[2]
    degrees = jnp.arange(degree_count, dtype=jnp.int32)
    retained = degrees[None, :] >= own_orders[:, None]
    spectrum = jnp.where(retained[:, None, :], love_gain[None, None, :] * degree_whole, 0.0)
    synthesis = jnp.einsum("krl,kcl->kcr", legendre, spectrum, precision=lax.Precision.HIGH)
    summed = inverse_dft(all_gather(synthesis, "lon"), slot_order, lon_start, lon_width, lon_total)
    loading = summed * (2 * slot_total) ** (-0.5)
    potential = masked - 0.6 * loading
    neighbours = neighbour_sum(potential)
    surface_next = wet_cells * (masked + 0.2 * (neighbours - 4.0 * potential))
    return (surface_next, loading)


def solution(mesh):
    return jax.shard_map(
        local,
        mesh=mesh,
        in_specs=(P("lat", "lon"), P("lat", "lon"), P("lon", "lat", None), P(), P()),
        out_specs=(P("lat", "lon"), P("lat", "lon")),
        check_vma=False,
    )
```

```python
import math

import jax
import jax.numpy as jnp
from jax import lax
from jax.sharding import PartitionSpec as P

BLK = 128


def halo(cells, axis, dim):
    count = lax.axis_size(axis)
    ends = count - 1
    head = lax.slice_in_dim(cells, 0, 1, axis=dim)
    tail = lax.slice_in_dim(cells, cells.shape[dim] - 1, cells.shape[dim], axis=dim)
    before = lax.ppermute(tail, axis, [(i, (i + 1) % count) for i in range(ends)])
    after = lax.ppermute(head, axis, [((i + 1) % count, i) for i in range(ends)])
    return before, after


def neighbour_sum(cells):
    up, down = halo(cells, "lat", 0)
    left, right = halo(cells, "lon", 1)
    rows = jnp.concatenate([up, cells[:-1]], axis=0) + jnp.concatenate([cells[1:], down], axis=0)
    cols = jnp.concatenate([left, cells[:, :-1]], axis=1) + jnp.concatenate([cells[:, 1:], right], axis=1)
    return rows + cols


INNER = 32


def dft_tables(order_count, lon_start, lon_width, lon_total):
    period = lon_total // INNER
    outer = jnp.arange(lon_width // INNER, dtype=jnp.int32)
    residue = jnp.arange(period, dtype=jnp.int32)
    alpha = (residue[:, None] * outer[None, :] % period).astype(jnp.float32) * (2.0 * math.pi / period)
    orders = jnp.arange(order_count, dtype=jnp.int32)
    inner = lon_start + jnp.arange(INNER, dtype=jnp.int32)
    beta = (orders[:, None] * inner[None, :] % lon_total).astype(jnp.float32) * (2.0 * math.pi / lon_total)
    beta = beta.reshape(order_count // period, period, INNER)
    return jnp.stack([jnp.cos(alpha), jnp.sin(alpha)]), jnp.cos(beta), jnp.sin(beta)


def forward_dft(masked, slot_order, lon_start, lon_total):
    cycles, lon_width = masked.shape
    order_count = slot_order.shape[0]
    rotor, cb, sb = dft_tables(order_count, lon_start, lon_width, lon_total)
    blocks = masked.reshape(cycles, lon_width // INNER, INNER)
    partial = jnp.einsum("cua,rab->cubr", rotor, blocks, precision=lax.Precision.HIGHEST)
    gc, gs = partial[0][None], partial[1][None]
    fc = (cb[..., None] * gc - sb[..., None] * gs).sum(axis=2)
    fs = (sb[..., None] * gc + cb[..., None] * gs).sum(axis=2)
    by_order = jnp.stack([fc, fs], axis=2).reshape(order_count, 2, cycles)
    return jnp.take(by_order, slot_order, axis=0, mode="clip", unique_indices=True)


def inverse_dft(synthesis, slot_order, lon_start, lon_width, lon_total):
    order_count, _, cycles = synthesis.shape
    rotor, cb, sb = dft_tables(order_count, lon_start, lon_width, lon_total)
    slots = jnp.arange(order_count, dtype=jnp.int32)
    slot_of = jnp.where(slot_order[None, :] == slots[:, None], slots[None, :], 0).sum(axis=1)
    by_order = jnp.take(synthesis, slot_of, axis=0, mode="clip", unique_indices=True).reshape(cb.shape[0], cb.shape[1], 2, cycles)
    yc, ys = by_order[:, :, 0, None, :], by_order[:, :, 1, None, :]
    hc = (yc * cb[..., None] + ys * sb[..., None]).sum(axis=0)
    hs = (ys * cb[..., None] - yc * sb[..., None]).sum(axis=0)
    out = jnp.einsum("cua,cubr->rab", rotor, jnp.stack([hc, hs]), precision=lax.Precision.HIGHEST)
    return out.reshape(cycles, lon_width)


def reduce_scatter(x, axis):
    count = lax.axis_size(axis)
    moved = lax.all_to_all(x, axis, 0, 0, tiled=True)
    return moved.reshape((count, x.shape[0] // count) + x.shape[1:]).sum(axis=0)


def all_gather(x, axis):
    count = lax.axis_size(axis)
    copies = jnp.broadcast_to(x[None], (count,) + x.shape).reshape((count * x.shape[0],) + x.shape[1:])
    return lax.all_to_all(copies, axis, 0, 0, tiled=True)


def halving_reduce_scatter(x, axis):
    count = lax.axis_size(axis)
    me = lax.axis_index(axis)
    step = 1
    while step < count:
        half = x.shape[0] // 2
        bit = me // step % 2
        kept = lax.dynamic_slice_in_dim(x, bit * half, half)
        sent = lax.dynamic_slice_in_dim(x, (1 - bit) * half, half)
        x = kept + lax.ppermute(sent, axis, [(i, i ^ step) for i in range(count)])
        step *= 2
    return x


def doubling_all_gather(x, axis):
    count = lax.axis_size(axis)
    me = lax.axis_index(axis)
    step = count // 2
    while step >= 1:
        bit = me // step % 2
        other = lax.ppermute(x, axis, [(i, i ^ step) for i in range(count)])
        x = jnp.where(bit == 0, jnp.concatenate([x, other]), jnp.concatenate([other, x]))
        step //= 2
    return x


def local(surface, wet_blocks, legendre, slot_order, love_gain):
    cycle_count, lon_width = surface.shape
    groups = lax.axis_size("lon")
    lon_total = lon_width * groups
    slot_count = legendre.shape[0]
    slot_total = slot_count * groups
    wet_cells = jnp.repeat(wet_blocks, BLK, axis=1).astype(jnp.float32)
    masked = wet_cells * surface
    lon_start = lax.axis_index("lon") * lon_width
    own_orders = lax.dynamic_slice_in_dim(
        slot_order, lax.axis_index("lon") * slot_count, slot_count
    )
    forward_scale = lon_total ** (-0.5)
    fourier = reduce_scatter(forward_dft(masked, slot_order, lon_start, lon_total) * forward_scale, "lon")
    coefficient = jnp.einsum("krl,kcr->kcl", legendre, fourier, precision=lax.Precision.HIGH)
    degree_whole = doubling_all_gather(halving_reduce_scatter(coefficient, "lat"), "lat")
    degree_count = degree_whole.shape[2]
    degrees = jnp.arange(degree_count, dtype=jnp.int32)
    retained = degrees[None, :] >= own_orders[:, None]
    spectrum = jnp.where(retained[:, None, :], love_gain[None, None, :] * degree_whole, 0.0)
    synthesis = jnp.einsum("krl,kcl->kcr", legendre, spectrum, precision=lax.Precision.HIGH)
    summed = inverse_dft(all_gather(synthesis, "lon"), slot_order, lon_start, lon_width, lon_total)
    loading = summed * (2 * slot_total) ** (-0.5)
    potential = masked - 0.6 * loading
    neighbours = neighbour_sum(potential)
    surface_next = wet_cells * (masked + 0.2 * (neighbours - 4.0 * potential))
    return (surface_next, loading)


def solution(mesh):
    return jax.shard_map(
        local,
        mesh=mesh,
        in_specs=(P("lat", "lon"), P("lat", "lon"), P("lon", "lat", None), P(), P()),
        out_specs=(P("lat", "lon"), P("lat", "lon")),
        check_vma=False,
    )
```

```python
import math

import jax
import jax.numpy as jnp
from jax import lax
from jax.sharding import PartitionSpec as P

BLK = 128


def halo(cells, axis, dim):
    count = lax.axis_size(axis)
    ends = count - 1
    head = lax.slice_in_dim(cells, 0, 1, axis=dim)
    tail = lax.slice_in_dim(cells, cells.shape[dim] - 1, cells.shape[dim], axis=dim)
    before = lax.ppermute(tail, axis, [(i, (i + 1) % count) for i in range(ends)])
    after = lax.ppermute(head, axis, [((i + 1) % count, i) for i in range(ends)])
    return before, after


def neighbour_sum(cells, left, right):
    up, down = halo(cells, "lat", 0)
    rows = jnp.concatenate([up, cells[:-1]], axis=0) + jnp.concatenate([cells[1:], down], axis=0)
    cols = jnp.concatenate([left, cells[:, :-1]], axis=1) + jnp.concatenate([cells[:, 1:], right], axis=1)
    return rows + cols


INNER = 32


def dft_tables(order_count, lon_start, lon_width, lon_total):
    period = lon_total // INNER
    outer = jnp.arange(lon_width // INNER, dtype=jnp.int32)
    residue = jnp.arange(period, dtype=jnp.int32)
    alpha = (residue[:, None] * outer[None, :] % period).astype(jnp.float32) * (2.0 * math.pi / period)
    orders = jnp.arange(order_count, dtype=jnp.int32)
    inner = lon_start + jnp.arange(INNER, dtype=jnp.int32)
    beta = (orders[:, None] * inner[None, :] % lon_total).astype(jnp.float32) * (2.0 * math.pi / lon_total)
    beta = beta.reshape(order_count // period, period, INNER)
    return jnp.stack([jnp.cos(alpha), jnp.sin(alpha)]), jnp.cos(beta), jnp.sin(beta)


def forward_dft(masked, slot_order, lon_start, lon_total):
    cycles, lon_width = masked.shape
    order_count = slot_order.shape[0]
    rotor, cb, sb = dft_tables(order_count, lon_start, lon_width, lon_total)
    blocks = masked.reshape(cycles, lon_width // INNER, INNER)
    partial = jnp.einsum("cua,rab->cubr", rotor, blocks, precision=lax.Precision.HIGHEST)
    gc, gs = partial[0][None], partial[1][None]
    fc = (cb[..., None] * gc - sb[..., None] * gs).sum(axis=2)
    fs = (sb[..., None] * gc + cb[..., None] * gs).sum(axis=2)
    by_order = jnp.stack([fc, fs], axis=2).reshape(order_count, 2, cycles)
    return jnp.take(by_order, slot_order, axis=0, mode="clip", unique_indices=True)


def inverse_dft(synthesis, slot_order, lon_start, lon_width, lon_total):
    order_count, _, cycles = synthesis.shape
    rotor, cb, sb = dft_tables(order_count, lon_start, lon_width, lon_total)
    slots = jnp.arange(order_count, dtype=jnp.int32)
    slot_of = jnp.where(slot_order[None, :] == slots[:, None], slots[None, :], 0).sum(axis=1)
    by_order = jnp.take(synthesis, slot_of, axis=0, mode="clip", unique_indices=True).reshape(cb.shape[0], cb.shape[1], 2, cycles)
    yc, ys = by_order[:, :, 0, None, :], by_order[:, :, 1, None, :]
    hc = (yc * cb[..., None] + ys * sb[..., None]).sum(axis=0)
    hs = (ys * cb[..., None] - yc * sb[..., None]).sum(axis=0)
    out = jnp.einsum("cua,cubr->rab", rotor, jnp.stack([hc, hs]), precision=lax.Precision.HIGHEST)
    return out.reshape(cycles, lon_width)


def reduce_scatter(x, axis):
    count = lax.axis_size(axis)
    moved = lax.all_to_all(x, axis, 0, 0, tiled=True)
    return moved.reshape((count, x.shape[0] // count) + x.shape[1:]).sum(axis=0)


def all_gather(x, axis):
    count = lax.axis_size(axis)
    copies = jnp.broadcast_to(x[None], (count,) + x.shape).reshape((count * x.shape[0],) + x.shape[1:])
    return lax.all_to_all(copies, axis, 0, 0, tiled=True)


def paired_reduce_scatter(x, axis):
    count = lax.axis_size(axis)
    pairs = [(i, i ^ 1) for i in range(count)]
    groups = [list(range(side, count, 2)) for side in (0, 1)]
    side = lax.axis_index(axis) % 2
    half = x.shape[0] // 2
    kept = lax.dynamic_slice_in_dim(x, side * half, half)
    sent = lax.dynamic_slice_in_dim(x, (1 - side) * half, half)
    summed = kept + lax.ppermute(sent, axis, pairs)
    moved = lax.all_to_all(summed, axis, 0, 0, tiled=True, axis_index_groups=groups)
    return moved.reshape((count // 2, half * 2 // count) + x.shape[1:]).sum(axis=0)


def paired_all_gather(x, axis):
    count = lax.axis_size(axis)
    pairs = [(i, i ^ 1) for i in range(count)]
    groups = [list(range(side, count, 2)) for side in (0, 1)]
    side = lax.axis_index(axis) % 2
    copies = jnp.broadcast_to(x[None], (count // 2,) + x.shape).reshape((count // 2 * x.shape[0],) + x.shape[1:])
    half = lax.all_to_all(copies, axis, 0, 0, tiled=True, axis_index_groups=groups)
    other = lax.ppermute(half, axis, pairs)
    return jnp.where(side == 0, jnp.concatenate([half, other]), jnp.concatenate([other, half]))


def local(surface, wet_blocks, legendre, slot_order, love_gain):
    cycle_count, lon_width = surface.shape
    groups = lax.axis_size("lon")
    lon_total = lon_width * groups
    slot_count = legendre.shape[0]
    slot_total = slot_count * groups
    wet_cells = jnp.repeat(wet_blocks, BLK, axis=1).astype(jnp.float32)
    masked = wet_cells * surface
    masked_left, masked_right = halo(masked, "lon", 1)
    lon_start = lax.axis_index("lon") * lon_width
    own_orders = lax.dynamic_slice_in_dim(
        slot_order, lax.axis_index("lon") * slot_count, slot_count
    )
    forward_scale = lon_total ** (-0.5)
    fourier = reduce_scatter(forward_dft(masked, slot_order, lon_start, lon_total) * forward_scale, "lon")
    coefficient = jnp.einsum("krl,kcr->kcl", legendre, fourier, precision=lax.Precision.HIGH)
    degree_whole = paired_all_gather(paired_reduce_scatter(coefficient, "lat"), "lat")
    degree_count = degree_whole.shape[2]
    degrees = jnp.arange(degree_count, dtype=jnp.int32)
    retained = degrees[None, :] >= own_orders[:, None]
    spectrum = jnp.where(retained[:, None, :], love_gain[None, None, :] * degree_whole, 0.0)
    synthesis = jnp.einsum("krl,kcl->kcr", legendre, spectrum, precision=lax.Precision.HIGH)
    inverse_scale = (2 * slot_total) ** (-0.5)
    gathered = all_gather(synthesis, "lon")
    loading = inverse_dft(gathered, slot_order, lon_start, lon_width, lon_total) * inverse_scale
    potential = masked - 0.6 * loading
    outside = jnp.array([-1, lon_width], dtype=jnp.int32)
    edge_angle = (slot_order[:, None] * ((lon_start + outside) % lon_total)[None, :] % lon_total).astype(jnp.float32)
    edge_angle = edge_angle * (2.0 * math.pi / lon_total)
    edge_table = jnp.stack([jnp.cos(edge_angle), jnp.sin(edge_angle)], axis=1)
    edge_loading = jnp.einsum("kcr,kcj->rj", gathered, edge_table, precision=lax.Precision.HIGHEST) * inverse_scale
    edge_potential = jnp.concatenate([masked_left, masked_right], axis=1) - 0.6 * edge_loading
    lon_index = lax.axis_index("lon")
    inside = jnp.stack([lon_index > 0, lon_index < groups - 1])[None, :]
    edge_potential = jnp.where(inside, edge_potential, 0.0)
    neighbours = neighbour_sum(potential, edge_potential[:, :1], edge_potential[:, 1:])
    surface_next = wet_cells * (masked + 0.2 * (neighbours - 4.0 * potential))
    return (surface_next, loading)


def solution(mesh):
    return jax.shard_map(
        local,
        mesh=mesh,
        in_specs=(P("lat", "lon"), P("lat", "lon"), P("lon", "lat", None), P(), P()),
        out_specs=(P("lat", "lon"), P("lat", "lon")),
        check_vma=False,
    )
```

```python
import math

import jax
import jax.numpy as jnp
from jax import lax
from jax.sharding import PartitionSpec as P

BLK = 128


def halo(cells, axis, dim):
    count = lax.axis_size(axis)
    ends = count - 1
    head = lax.slice_in_dim(cells, 0, 1, axis=dim)
    tail = lax.slice_in_dim(cells, cells.shape[dim] - 1, cells.shape[dim], axis=dim)
    before = lax.ppermute(tail, axis, [(i, (i + 1) % count) for i in range(ends)])
    after = lax.ppermute(head, axis, [((i + 1) % count, i) for i in range(ends)])
    return before, after


def neighbour_sum(cells):
    up, down = halo(cells, "lat", 0)
    left, right = halo(cells, "lon", 1)
    rows = jnp.concatenate([up, cells[:-1]], axis=0) + jnp.concatenate([cells[1:], down], axis=0)
    cols = jnp.concatenate([left, cells[:, :-1]], axis=1) + jnp.concatenate([cells[:, 1:], right], axis=1)
    return rows + cols


INNER = 32


def dft_tables(order_count, lon_start, lon_width, lon_total):
    period = lon_total // INNER
    outer = jnp.arange(lon_width // INNER, dtype=jnp.int32)
    residue = jnp.arange(period, dtype=jnp.int32)
    alpha = (residue[:, None] * outer[None, :] % period).astype(jnp.float32) * (2.0 * math.pi / period)
    orders = jnp.arange(order_count, dtype=jnp.int32)
    inner = lon_start + jnp.arange(INNER, dtype=jnp.int32)
    beta = (orders[:, None] * inner[None, :] % lon_total).astype(jnp.float32) * (2.0 * math.pi / lon_total)
    beta = beta.reshape(order_count // period, period, INNER)
    return jnp.stack([jnp.cos(alpha), jnp.sin(alpha)]), jnp.cos(beta), jnp.sin(beta)


def forward_dft(masked, slot_order, lon_start, lon_total):
    cycles, lon_width = masked.shape
    order_count = slot_order.shape[0]
    rotor, cb, sb = dft_tables(order_count, lon_start, lon_width, lon_total)
    blocks = masked.reshape(cycles, lon_width // INNER, INNER)
    partial = jnp.einsum("cua,rab->cubr", rotor, blocks, precision=lax.Precision.HIGHEST)
    gc, gs = partial[0][None], partial[1][None]
    fc = (cb[..., None] * gc - sb[..., None] * gs).sum(axis=2)
    fs = (sb[..., None] * gc + cb[..., None] * gs).sum(axis=2)
    by_order = jnp.stack([fc, fs], axis=2).reshape(order_count, 2, cycles)
    return jnp.take(by_order, slot_order, axis=0, mode="clip", unique_indices=True)


def inverse_dft(synthesis, slot_order, lon_start, lon_width, lon_total):
    order_count, _, cycles = synthesis.shape
    rotor, cb, sb = dft_tables(order_count, lon_start, lon_width, lon_total)
    slots = jnp.arange(order_count, dtype=jnp.int32)
    slot_of = jnp.where(slot_order[None, :] == slots[:, None], slots[None, :], 0).sum(axis=1)
    by_order = jnp.take(synthesis, slot_of, axis=0, mode="clip", unique_indices=True).reshape(cb.shape[0], cb.shape[1], 2, cycles)
    yc, ys = by_order[:, :, 0, None, :], by_order[:, :, 1, None, :]
    hc = (yc * cb[..., None] + ys * sb[..., None]).sum(axis=0)
    hs = (ys * cb[..., None] - yc * sb[..., None]).sum(axis=0)
    out = jnp.einsum("cua,cubr->rab", rotor, jnp.stack([hc, hs]), precision=lax.Precision.HIGHEST)
    return out.reshape(cycles, lon_width)


def reduce_scatter(x, axis):
    count = lax.axis_size(axis)
    moved = lax.all_to_all(x, axis, 0, 0, tiled=True)
    return moved.reshape((count, x.shape[0] // count) + x.shape[1:]).sum(axis=0)


def all_gather(x, axis):
    count = lax.axis_size(axis)
    copies = jnp.broadcast_to(x[None], (count,) + x.shape).reshape((count * x.shape[0],) + x.shape[1:])
    return lax.all_to_all(copies, axis, 0, 0, tiled=True)


def paired_reduce_scatter(x, axis):
    count = lax.axis_size(axis)
    pairs = [(i, i ^ 1) for i in range(count)]
    groups = [list(range(side, count, 2)) for side in (0, 1)]
    side = lax.axis_index(axis) % 2
    half = x.shape[0] // 2
    kept = lax.dynamic_slice_in_dim(x, side * half, half)
    sent = lax.dynamic_slice_in_dim(x, (1 - side) * half, half)
    summed = kept + lax.ppermute(sent, axis, pairs)
    moved = lax.all_to_all(summed, axis, 0, 0, tiled=True, axis_index_groups=groups)
    return moved.reshape((count // 2, half * 2 // count) + x.shape[1:]).sum(axis=0)


def paired_all_gather(x, axis):
    count = lax.axis_size(axis)
    pairs = [(i, i ^ 1) for i in range(count)]
    groups = [list(range(side, count, 2)) for side in (0, 1)]
    side = lax.axis_index(axis) % 2
    copies = jnp.broadcast_to(x[None], (count // 2,) + x.shape).reshape((count // 2 * x.shape[0],) + x.shape[1:])
    half = lax.all_to_all(copies, axis, 0, 0, tiled=True, axis_index_groups=groups)
    other = lax.ppermute(half, axis, pairs)
    return jnp.where(side == 0, jnp.concatenate([half, other]), jnp.concatenate([other, half]))


def local(surface, wet_blocks, legendre, slot_order, love_gain):
    cycle_count, lon_width = surface.shape
    groups = lax.axis_size("lon")
    lon_total = lon_width * groups
    slot_count = legendre.shape[0]
    slot_total = slot_count * groups
    wet_cells = jnp.repeat(wet_blocks, BLK, axis=1).astype(jnp.float32)
    masked = wet_cells * surface
    lon_start = lax.axis_index("lon") * lon_width
    own_orders = lax.dynamic_slice_in_dim(
        slot_order, lax.axis_index("lon") * slot_count, slot_count
    )
    forward_scale = lon_total ** (-0.5)
    fourier = reduce_scatter(forward_dft(masked, slot_order, lon_start, lon_total) * forward_scale, "lon")
    coefficient = jnp.einsum("krl,kcr->kcl", legendre, fourier, precision=lax.Precision.HIGH)
    degree_whole = paired_all_gather(paired_reduce_scatter(coefficient, "lat"), "lat")
    degree_count = degree_whole.shape[2]
    degrees = jnp.arange(degree_count, dtype=jnp.int32)
    retained = degrees[None, :] >= own_orders[:, None]
    spectrum = jnp.where(retained[:, None, :], love_gain[None, None, :] * degree_whole, 0.0)
    synthesis = (legendre[:, None, :, :] * spectrum[:, :, None, :]).sum(axis=3)
    summed = inverse_dft(all_gather(synthesis, "lon"), slot_order, lon_start, lon_width, lon_total)
    loading = summed * (2 * slot_total) ** (-0.5)
    potential = masked - 0.6 * loading
    neighbours = neighbour_sum(potential)
    surface_next = wet_cells * (masked + 0.2 * (neighbours - 4.0 * potential))
    return (surface_next, loading)


def solution(mesh):
    return jax.shard_map(
        local,
        mesh=mesh,
        in_specs=(P("lat", "lon"), P("lat", "lon"), P("lon", "lat", None), P(), P()),
        out_specs=(P("lat", "lon"), P("lat", "lon")),
        check_vma=False,
    )
```

```python
import math

import jax
import jax.numpy as jnp
from jax import lax
from jax.sharding import PartitionSpec as P

BLK = 128


def halo(cells, axis, dim):
    count = lax.axis_size(axis)
    ends = count - 1
    head = lax.slice_in_dim(cells, 0, 1, axis=dim)
    tail = lax.slice_in_dim(cells, cells.shape[dim] - 1, cells.shape[dim], axis=dim)
    before = lax.ppermute(tail, axis, [(i, (i + 1) % count) for i in range(ends)])
    after = lax.ppermute(head, axis, [((i + 1) % count, i) for i in range(ends)])
    return before, after


def neighbour_sum(cells):
    up, down = halo(cells, "lat", 0)
    left, right = halo(cells, "lon", 1)
    rows = jnp.concatenate([up, cells[:-1]], axis=0) + jnp.concatenate([cells[1:], down], axis=0)
    cols = jnp.concatenate([left, cells[:, :-1]], axis=1) + jnp.concatenate([cells[:, 1:], right], axis=1)
    return rows + cols


INNER = 32


def dft_tables(order_count, lon_start, lon_width, lon_total):
    period = lon_total // INNER
    outer = jnp.arange(lon_width // INNER, dtype=jnp.int32)
    residue = jnp.arange(period, dtype=jnp.int32)
    alpha = (residue[:, None] * outer[None, :] % period).astype(jnp.float32) * (2.0 * math.pi / period)
    orders = jnp.arange(order_count, dtype=jnp.int32)
    inner = lon_start + jnp.arange(INNER, dtype=jnp.int32)
    beta = (orders[:, None] * inner[None, :] % lon_total).astype(jnp.float32) * (2.0 * math.pi / lon_total)
    beta = beta.reshape(order_count // period, period, INNER)
    return jnp.stack([jnp.cos(alpha), jnp.sin(alpha)]), jnp.cos(beta), jnp.sin(beta)


def forward_dft(masked, slot_order, lon_start, lon_total):
    cycles, lon_width = masked.shape
    order_count = slot_order.shape[0]
    rotor, cb, sb = dft_tables(order_count, lon_start, lon_width, lon_total)
    blocks = masked.reshape(cycles, lon_width // INNER, INNER)
    partial = jnp.einsum("cua,rab->cubr", rotor, blocks, precision=lax.Precision.HIGHEST)
    gc, gs = partial[0][None], partial[1][None]
    fc = (cb[..., None] * gc - sb[..., None] * gs).sum(axis=2)
    fs = (sb[..., None] * gc + cb[..., None] * gs).sum(axis=2)
    by_order = jnp.stack([fc, fs], axis=2).reshape(order_count, 2, cycles)
    return jnp.take(by_order, slot_order, axis=0, mode="clip", unique_indices=True)


def inverse_dft(synthesis, slot_order, lon_start, lon_width, lon_total):
    order_count, _, cycles = synthesis.shape
    rotor, cb, sb = dft_tables(order_count, lon_start, lon_width, lon_total)
    slots = jnp.arange(order_count, dtype=jnp.int32)
    slot_of = jnp.where(slot_order[None, :] == slots[:, None], slots[None, :], 0).sum(axis=1)
    by_order = jnp.take(synthesis, slot_of, axis=0, mode="clip", unique_indices=True).reshape(cb.shape[0], cb.shape[1], 2, cycles)
    yc, ys = by_order[:, :, 0, None, :], by_order[:, :, 1, None, :]
    hc = (yc * cb[..., None] + ys * sb[..., None]).sum(axis=0)
    hs = (ys * cb[..., None] - yc * sb[..., None]).sum(axis=0)
    out = jnp.einsum("cua,cubr->rab", rotor, jnp.stack([hc, hs]), precision=lax.Precision.HIGHEST)
    return out.reshape(cycles, lon_width)


def reduce_scatter(x, axis):
    count = lax.axis_size(axis)
    moved = lax.all_to_all(x, axis, 0, 0, tiled=True)
    return moved.reshape((count, x.shape[0] // count) + x.shape[1:]).sum(axis=0)


def all_gather(x, axis):
    count = lax.axis_size(axis)
    copies = jnp.broadcast_to(x[None], (count,) + x.shape).reshape((count * x.shape[0],) + x.shape[1:])
    return lax.all_to_all(copies, axis, 0, 0, tiled=True)


def paired_reduce_scatter(x, axis):
    count = lax.axis_size(axis)
    pairs = [(i, i ^ 1) for i in range(count)]
    groups = [list(range(side, count, 2)) for side in (0, 1)]
    side = lax.axis_index(axis) % 2
    half = x.shape[0] // 2
    kept = lax.dynamic_slice_in_dim(x, side * half, half)
    sent = lax.dynamic_slice_in_dim(x, (1 - side) * half, half)
    summed = kept + lax.ppermute(sent, axis, pairs)
    moved = lax.all_to_all(summed, axis, 0, 0, tiled=True, axis_index_groups=groups)
    return moved.reshape((count // 2, half * 2 // count) + x.shape[1:]).sum(axis=0)


def paired_all_gather(x, axis):
    count = lax.axis_size(axis)
    pairs = [(i, i ^ 1) for i in range(count)]
    groups = [list(range(side, count, 2)) for side in (0, 1)]
    side = lax.axis_index(axis) % 2
    copies = jnp.broadcast_to(x[None], (count // 2,) + x.shape).reshape((count // 2 * x.shape[0],) + x.shape[1:])
    half = lax.all_to_all(copies, axis, 0, 0, tiled=True, axis_index_groups=groups)
    other = lax.ppermute(half, axis, pairs)
    return jnp.where(side == 0, jnp.concatenate([half, other]), jnp.concatenate([other, half]))


def local(surface, wet_blocks, legendre, slot_order, love_gain):
    cycle_count, lon_width = surface.shape
    groups = lax.axis_size("lon")
    lon_total = lon_width * groups
    slot_count = legendre.shape[0]
    slot_total = slot_count * groups
    wet_cells = jnp.repeat(wet_blocks, BLK, axis=1).astype(jnp.float32)
    masked = wet_cells * surface
    lon_start = lax.axis_index("lon") * lon_width
    own_orders = lax.dynamic_slice_in_dim(
        slot_order, lax.axis_index("lon") * slot_count, slot_count
    )
    forward_scale = lon_total ** (-0.5)
    fourier = reduce_scatter(forward_dft(masked, slot_order, lon_start, lon_total) * forward_scale, "lon")
    coefficient = jnp.einsum("krl,kcr->kcl", legendre, fourier, precision=lax.Precision.HIGH)
    degree_part = paired_reduce_scatter(coefficient, "lat")
    lat_count = lax.axis_size("lat")
    lat_index = lax.axis_index("lat")
    half = slot_count // 2
    part = degree_part.shape[0]
    part_orders = lax.dynamic_slice_in_dim(own_orders, lat_index % 2 * half + lat_index // 2 * part, part)
    degrees = jnp.arange(degree_part.shape[2], dtype=jnp.int32)
    retained = degrees[None, :] >= part_orders[:, None]
    spectrum = paired_all_gather(
        jnp.where(retained[:, None, :], love_gain[None, None, :] * degree_part, 0.0), "lat"
    )
    synthesis = (legendre[:, None, :, :] * spectrum[:, :, None, :]).sum(axis=3)
    summed = inverse_dft(all_gather(synthesis, "lon"), slot_order, lon_start, lon_width, lon_total)
    loading = summed * (2 * slot_total) ** (-0.5)
    potential = masked - 0.6 * loading
    neighbours = neighbour_sum(potential)
    surface_next = wet_cells * (masked + 0.2 * (neighbours - 4.0 * potential))
    return (surface_next, loading)


def solution(mesh):
    return jax.shard_map(
        local,
        mesh=mesh,
        in_specs=(P("lat", "lon"), P("lat", "lon"), P("lon", "lat", None), P(), P()),
        out_specs=(P("lat", "lon"), P("lat", "lon")),
        check_vma=False,
    )
```

```python
import math

import jax
import jax.numpy as jnp
from jax import lax
from jax.sharding import PartitionSpec as P

BLK = 128


def halo(cells, axis, dim):
    count = lax.axis_size(axis)
    ends = count - 1
    head = lax.slice_in_dim(cells, 0, 1, axis=dim)
    tail = lax.slice_in_dim(cells, cells.shape[dim] - 1, cells.shape[dim], axis=dim)
    before = lax.ppermute(tail, axis, [(i, (i + 1) % count) for i in range(ends)])
    after = lax.ppermute(head, axis, [((i + 1) % count, i) for i in range(ends)])
    return before, after


def neighbour_sum(cells):
    up, down = halo(cells, "lat", 0)
    left, right = halo(cells, "lon", 1)
    rows = jnp.concatenate([up, cells[:-1]], axis=0) + jnp.concatenate([cells[1:], down], axis=0)
    cols = jnp.concatenate([left, cells[:, :-1]], axis=1) + jnp.concatenate([cells[:, 1:], right], axis=1)
    return rows + cols


INNER = 32


def dft_tables(order_count, lon_start, lon_width, lon_total):
    period = lon_total // INNER
    outer = jnp.arange(lon_width // INNER, dtype=jnp.int32)
    residue = jnp.arange(period, dtype=jnp.int32)
    alpha = (residue[:, None] * outer[None, :] % period).astype(jnp.float32) * (2.0 * math.pi / period)
    orders = jnp.arange(order_count, dtype=jnp.int32)
    inner = lon_start + jnp.arange(INNER, dtype=jnp.int32)
    beta = (orders[:, None] * inner[None, :] % lon_total).astype(jnp.float32) * (2.0 * math.pi / lon_total)
    beta = beta.reshape(order_count // period, period, INNER)
    return jnp.stack([jnp.cos(alpha), jnp.sin(alpha)]), jnp.cos(beta), jnp.sin(beta)


def forward_dft(masked, slot_order, lon_start, lon_total):
    cycles, lon_width = masked.shape
    order_count = slot_order.shape[0]
    rotor, cb, sb = dft_tables(order_count, lon_start, lon_width, lon_total)
    blocks = masked.reshape(cycles, lon_width // INNER, INNER)
    partial = jnp.einsum("cua,rab->cubr", rotor, blocks, precision=lax.Precision.HIGHEST)
    gc, gs = partial[0][None], partial[1][None]
    fc = (cb[..., None] * gc - sb[..., None] * gs).sum(axis=2)
    fs = (sb[..., None] * gc + cb[..., None] * gs).sum(axis=2)
    by_order = jnp.stack([fc, fs], axis=2).reshape(order_count, 2, cycles)
    return jnp.take(by_order, slot_order, axis=0, mode="clip", unique_indices=True)


def inverse_dft(synthesis, slot_order, lon_start, lon_width, lon_total):
    order_count, _, cycles = synthesis.shape
    rotor, cb, sb = dft_tables(order_count, lon_start, lon_width, lon_total)
    slots = jnp.arange(order_count, dtype=jnp.int32)
    slot_of = jnp.where(slot_order[None, :] == slots[:, None], slots[None, :], 0).sum(axis=1)
    by_order = jnp.take(synthesis, slot_of, axis=0, mode="clip", unique_indices=True).reshape(cb.shape[0], cb.shape[1], 2, cycles)
    yc, ys = by_order[:, :, 0, None, :], by_order[:, :, 1, None, :]
    hc = (yc * cb[..., None] + ys * sb[..., None]).sum(axis=0)
    hs = (ys * cb[..., None] - yc * sb[..., None]).sum(axis=0)
    out = jnp.einsum("cua,cubr->rab", rotor, jnp.stack([hc, hs]), precision=lax.Precision.HIGHEST)
    return out.reshape(cycles, lon_width)


def reduce_scatter(x, axis):
    count = lax.axis_size(axis)
    moved = lax.all_to_all(x, axis, 0, 0, tiled=True)
    return moved.reshape((count, x.shape[0] // count) + x.shape[1:]).sum(axis=0)


def all_gather(x, axis):
    count = lax.axis_size(axis)
    copies = jnp.broadcast_to(x[None], (count,) + x.shape).reshape((count * x.shape[0],) + x.shape[1:])
    return lax.all_to_all(copies, axis, 0, 0, tiled=True)


def paired_reduce_scatter(x, axis):
    count = lax.axis_size(axis)
    pairs = [(i, i ^ 1) for i in range(count)]
    groups = [list(range(side, count, 2)) for side in (0, 1)]
    side = lax.axis_index(axis) % 2
    half = x.shape[0] // 2
    kept = lax.dynamic_slice_in_dim(x, side * half, half)
    sent = lax.dynamic_slice_in_dim(x, (1 - side) * half, half)
    summed = kept + lax.ppermute(sent, axis, pairs)
    moved = lax.all_to_all(summed, axis, 0, 0, tiled=True, axis_index_groups=groups)
    return moved.reshape((count // 2, half * 2 // count) + x.shape[1:]).sum(axis=0)


def paired_all_gather(x, axis):
    count = lax.axis_size(axis)
    pairs = [(i, i ^ 1) for i in range(count)]
    groups = [list(range(side, count, 2)) for side in (0, 1)]
    side = lax.axis_index(axis) % 2
    copies = jnp.broadcast_to(x[None], (count // 2,) + x.shape).reshape((count // 2 * x.shape[0],) + x.shape[1:])
    half = lax.all_to_all(copies, axis, 0, 0, tiled=True, axis_index_groups=groups)
    other = lax.ppermute(half, axis, pairs)
    return jnp.where(side == 0, jnp.concatenate([half, other]), jnp.concatenate([other, half]))


def local(surface, wet_blocks, legendre, slot_order, love_gain):
    cycle_count, lon_width = surface.shape
    groups = lax.axis_size("lon")
    lon_total = lon_width * groups
    slot_count = legendre.shape[0]
    slot_total = slot_count * groups
    wet_cells = jnp.repeat(wet_blocks, BLK, axis=1).astype(jnp.float32)
    masked = wet_cells * surface
    lon_start = lax.axis_index("lon") * lon_width
    own_orders = lax.dynamic_slice_in_dim(
        slot_order, lax.axis_index("lon") * slot_count, slot_count
    )
    forward_scale = lon_total ** (-0.5)
    fourier = reduce_scatter(forward_dft(masked, slot_order, lon_start, lon_total) * forward_scale, "lon")
    coefficient = jnp.einsum("krl,kcr->kcl", legendre, fourier, precision=lax.Precision.HIGH)
    degree_whole = paired_all_gather(paired_reduce_scatter(coefficient, "lat"), "lat")
    degree_count = degree_whole.shape[2]
    degrees = jnp.arange(degree_count, dtype=jnp.int32)
    retained = degrees[None, :] >= own_orders[:, None]
    spectrum = jnp.where(retained[:, None, :], love_gain[None, None, :] * degree_whole, 0.0)
    synthesis = (legendre[:, None, :, :] * spectrum[:, :, None, :]).sum(axis=3)
    summed = inverse_dft(lax.all_gather(synthesis, "lon", axis=0, tiled=True), slot_order, lon_start, lon_width, lon_total)
    loading = summed * (2 * slot_total) ** (-0.5)
    potential = masked - 0.6 * loading
    neighbours = neighbour_sum(potential)
    surface_next = wet_cells * (masked + 0.2 * (neighbours - 4.0 * potential))
    return (surface_next, loading)


def solution(mesh):
    return jax.shard_map(
        local,
        mesh=mesh,
        in_specs=(P("lat", "lon"), P("lat", "lon"), P("lon", "lat", None), P(), P()),
        out_specs=(P("lat", "lon"), P("lat", "lon")),
        check_vma=False,
    )
```

```python
import math

import jax
import jax.numpy as jnp
from jax import lax
from jax.sharding import PartitionSpec as P

BLK = 128


def halo(cells, axis, dim):
    count = lax.axis_size(axis)
    ends = count - 1
    head = lax.slice_in_dim(cells, 0, 1, axis=dim)
    tail = lax.slice_in_dim(cells, cells.shape[dim] - 1, cells.shape[dim], axis=dim)
    before = lax.ppermute(tail, axis, [(i, (i + 1) % count) for i in range(ends)])
    after = lax.ppermute(head, axis, [((i + 1) % count, i) for i in range(ends)])
    return before, after


def neighbour_sum(cells):
    up, down = halo(cells, "lat", 0)
    left, right = halo(cells, "lon", 1)
    rows = jnp.concatenate([up, cells[:-1]], axis=0) + jnp.concatenate([cells[1:], down], axis=0)
    cols = jnp.concatenate([left, cells[:, :-1]], axis=1) + jnp.concatenate([cells[:, 1:], right], axis=1)
    return rows + cols


INNER = 32


def dft_tables(order_count, lon_start, lon_width, lon_total):
    period = lon_total // INNER
    outer = jnp.arange(lon_width // INNER, dtype=jnp.int32)
    residue = jnp.arange(period, dtype=jnp.int32)
    alpha = (residue[:, None] * outer[None, :] % period).astype(jnp.float32) * (2.0 * math.pi / period)
    orders = jnp.arange(order_count, dtype=jnp.int32)
    inner = lon_start + jnp.arange(INNER, dtype=jnp.int32)
    beta = (orders[:, None] * inner[None, :] % lon_total).astype(jnp.float32) * (2.0 * math.pi / lon_total)
    beta = beta.reshape(order_count // period, period, INNER)
    return jnp.stack([jnp.cos(alpha), jnp.sin(alpha)]), jnp.cos(beta), jnp.sin(beta)


def forward_dft(masked, slot_order, order_count, lon_start, lon_total):
    cycles, lon_width = masked.shape
    rotor, cb, sb = dft_tables(order_count, lon_start, lon_width, lon_total)
    blocks = masked.reshape(cycles, lon_width // INNER, INNER)
    partial = jnp.einsum("cua,rab->cubr", rotor, blocks, precision=lax.Precision.HIGHEST)
    gc, gs = partial[0][None], partial[1][None]
    fc = (cb[..., None] * gc - sb[..., None] * gs).sum(axis=2)
    fs = (sb[..., None] * gc + cb[..., None] * gs).sum(axis=2)
    by_order = jnp.stack([fc, fs], axis=2).reshape(order_count, 2, cycles)
    return jnp.take(by_order, slot_order, axis=0, mode="clip", unique_indices=True)


def inverse_dft(synthesis, slot_order, lon_start, lon_width, lon_total):
    order_count, _, cycles = synthesis.shape
    rotor, cb, sb = dft_tables(order_count, lon_start, lon_width, lon_total)
    slots = jnp.arange(order_count, dtype=jnp.int32)
    slot_of = jnp.where(slot_order[None, :] == slots[:, None], slots[None, :], 0).sum(axis=1)
    by_order = jnp.take(synthesis, slot_of, axis=0, mode="clip", unique_indices=True).reshape(cb.shape[0], cb.shape[1], 2, cycles)
    yc, ys = by_order[:, :, 0, None, :], by_order[:, :, 1, None, :]
    hc = (yc * cb[..., None] + ys * sb[..., None]).sum(axis=0)
    hs = (ys * cb[..., None] - yc * sb[..., None]).sum(axis=0)
    out = jnp.einsum("cua,cubr->rab", rotor, jnp.stack([hc, hs]), precision=lax.Precision.HIGHEST)
    return out.reshape(cycles, lon_width)


def reduce_scatter(x, axis):
    count = lax.axis_size(axis)
    moved = lax.all_to_all(x, axis, 0, 0, tiled=True)
    return moved.reshape((count, x.shape[0] // count) + x.shape[1:]).sum(axis=0)


def all_gather(x, axis):
    count = lax.axis_size(axis)
    copies = jnp.broadcast_to(x[None], (count,) + x.shape).reshape((count * x.shape[0],) + x.shape[1:])
    return lax.all_to_all(copies, axis, 0, 0, tiled=True)


def paired_reduce_scatter(x, axis):
    count = lax.axis_size(axis)
    pairs = [(i, i ^ 1) for i in range(count)]
    groups = [list(range(side, count, 2)) for side in (0, 1)]
    side = lax.axis_index(axis) % 2
    half = x.shape[0] // 2
    kept = lax.dynamic_slice_in_dim(x, side * half, half)
    sent = lax.dynamic_slice_in_dim(x, (1 - side) * half, half)
    summed = kept + lax.ppermute(sent, axis, pairs)
    moved = lax.all_to_all(summed, axis, 0, 0, tiled=True, axis_index_groups=groups)
    return moved.reshape((count // 2, half * 2 // count) + x.shape[1:]).sum(axis=0)


def paired_all_gather(x, axis):
    count = lax.axis_size(axis)
    pairs = [(i, i ^ 1) for i in range(count)]
    groups = [list(range(side, count, 2)) for side in (0, 1)]
    side = lax.axis_index(axis) % 2
    copies = jnp.broadcast_to(x[None], (count // 2,) + x.shape).reshape((count // 2 * x.shape[0],) + x.shape[1:])
    half = lax.all_to_all(copies, axis, 0, 0, tiled=True, axis_index_groups=groups)
    other = lax.ppermute(half, axis, pairs)
    return jnp.where(side == 0, jnp.concatenate([half, other]), jnp.concatenate([other, half]))


def local(surface, wet_blocks, legendre, slot_order, love_gain):
    cycle_count, lon_width = surface.shape
    groups = lax.axis_size("lon")
    lon_total = lon_width * groups
    slot_count = legendre.shape[0]
    slot_total = slot_count * groups
    wet_cells = jnp.repeat(wet_blocks, BLK, axis=1).astype(jnp.float32)
    masked = wet_cells * surface
    lon_start = lax.axis_index("lon") * lon_width
    own_orders = lax.dynamic_slice_in_dim(
        slot_order, lax.axis_index("lon") * slot_count, slot_count
    )
    forward_scale = lon_total ** (-0.5)
    masked_row = lax.all_gather(masked, "lon", axis=1, tiled=True)
    fourier = forward_dft(masked_row, own_orders, slot_total, 0, lon_total) * forward_scale
    coefficient = jnp.einsum("krl,kcr->kcl", legendre, fourier, precision=lax.Precision.HIGH)
    degree_whole = paired_all_gather(paired_reduce_scatter(coefficient, "lat"), "lat")
    degree_count = degree_whole.shape[2]
    degrees = jnp.arange(degree_count, dtype=jnp.int32)
    retained = degrees[None, :] >= own_orders[:, None]
    spectrum = jnp.where(retained[:, None, :], love_gain[None, None, :] * degree_whole, 0.0)
    synthesis = (legendre[:, None, :, :] * spectrum[:, :, None, :]).sum(axis=3)
    summed = inverse_dft(lax.all_gather(synthesis, "lon", axis=0, tiled=True), slot_order, lon_start, lon_width, lon_total)
    loading = summed * (2 * slot_total) ** (-0.5)
    potential = masked - 0.6 * loading
    neighbours = neighbour_sum(potential)
    surface_next = wet_cells * (masked + 0.2 * (neighbours - 4.0 * potential))
    return (surface_next, loading)


def solution(mesh):
    return jax.shard_map(
        local,
        mesh=mesh,
        in_specs=(P("lat", "lon"), P("lat", "lon"), P("lon", "lat", None), P(), P()),
        out_specs=(P("lat", "lon"), P("lat", "lon")),
        check_vma=False,
    )
```

```python
import math

import jax
import jax.numpy as jnp
from jax import lax
from jax.sharding import PartitionSpec as P

BLK = 128


def halo(cells, axis, dim):
    count = lax.axis_size(axis)
    ends = count - 1
    head = lax.slice_in_dim(cells, 0, 1, axis=dim)
    tail = lax.slice_in_dim(cells, cells.shape[dim] - 1, cells.shape[dim], axis=dim)
    before = lax.ppermute(tail, axis, [(i, (i + 1) % count) for i in range(ends)])
    after = lax.ppermute(head, axis, [((i + 1) % count, i) for i in range(ends)])
    return before, after


def neighbour_sum(cells):
    up, down = halo(cells, "lat", 0)
    left, right = halo(cells, "lon", 1)
    rows = jnp.concatenate([up, cells[:-1]], axis=0) + jnp.concatenate([cells[1:], down], axis=0)
    cols = jnp.concatenate([left, cells[:, :-1]], axis=1) + jnp.concatenate([cells[:, 1:], right], axis=1)
    return rows + cols


INNER = 32


def dft_tables(order_count, lon_start, lon_width, lon_total):
    period = lon_total // INNER
    outer = jnp.arange(lon_width // INNER, dtype=jnp.int32)
    residue = jnp.arange(period, dtype=jnp.int32)
    alpha = (residue[:, None] * outer[None, :] % period).astype(jnp.float32) * (2.0 * math.pi / period)
    orders = jnp.arange(order_count, dtype=jnp.int32)
    inner = lon_start + jnp.arange(INNER, dtype=jnp.int32)
    beta = (orders[:, None] * inner[None, :] % lon_total).astype(jnp.float32) * (2.0 * math.pi / lon_total)
    beta = beta.reshape(order_count // period, period, INNER)
    return jnp.stack([jnp.cos(alpha), jnp.sin(alpha)]), jnp.cos(beta), jnp.sin(beta)


def forward_dft(masked, slot_order, lon_start, lon_total):
    cycles, lon_width = masked.shape
    order_count = slot_order.shape[0]
    rotor, cb, sb = dft_tables(order_count, lon_start, lon_width, lon_total)
    blocks = masked.reshape(cycles, lon_width // INNER, INNER)
    partial = jnp.einsum("cua,rab->cubr", rotor, blocks, precision=lax.Precision.HIGHEST)
    gc, gs = partial[0][None], partial[1][None]
    fc = (cb[..., None] * gc - sb[..., None] * gs).sum(axis=2)
    fs = (sb[..., None] * gc + cb[..., None] * gs).sum(axis=2)
    by_order = jnp.stack([fc, fs], axis=2).reshape(order_count, 2 * cycles)
    return jnp.take(by_order, slot_order, axis=0, mode="clip", unique_indices=True)


def inverse_dft(synthesis, slot_order, lon_start, lon_width, lon_total):
    order_count, _, cycles = synthesis.shape
    rotor, cb, sb = dft_tables(order_count, lon_start, lon_width, lon_total)
    slots = jnp.arange(order_count, dtype=jnp.int32)
    slot_of = jnp.where(slot_order[None, :] == slots[:, None], slots[None, :], 0).sum(axis=1)
    by_order = jnp.take(synthesis, slot_of, axis=0, mode="clip", unique_indices=True).reshape(cb.shape[0], cb.shape[1], 2, cycles)
    yc, ys = by_order[:, :, 0, None, :], by_order[:, :, 1, None, :]
    hc = (yc * cb[..., None] + ys * sb[..., None]).sum(axis=0)
    hs = (ys * cb[..., None] - yc * sb[..., None]).sum(axis=0)
    out = jnp.einsum("cua,cubr->rab", rotor, jnp.stack([hc, hs]), precision=lax.Precision.HIGHEST)
    return out.reshape(cycles, lon_width)


def reduce_scatter(x, axis):
    count = lax.axis_size(axis)
    moved = lax.all_to_all(x, axis, 0, 0, tiled=True)
    return moved.reshape((count, x.shape[0] // count) + x.shape[1:]).sum(axis=0)


def all_gather(x, axis):
    count = lax.axis_size(axis)
    copies = jnp.broadcast_to(x[None], (count,) + x.shape).reshape((count * x.shape[0],) + x.shape[1:])
    return lax.all_to_all(copies, axis, 0, 0, tiled=True)


def paired_reduce_scatter(x, axis):
    count = lax.axis_size(axis)
    pairs = [(i, i ^ 1) for i in range(count)]
    groups = [list(range(side, count, 2)) for side in (0, 1)]
    side = lax.axis_index(axis) % 2
    half = x.shape[0] // 2
    kept = lax.dynamic_slice_in_dim(x, side * half, half)
    sent = lax.dynamic_slice_in_dim(x, (1 - side) * half, half)
    summed = kept + lax.ppermute(sent, axis, pairs)
    moved = lax.all_to_all(summed, axis, 0, 0, tiled=True, axis_index_groups=groups)
    return moved.reshape((count // 2, half * 2 // count) + x.shape[1:]).sum(axis=0)


def paired_all_gather(x, axis):
    count = lax.axis_size(axis)
    pairs = [(i, i ^ 1) for i in range(count)]
    groups = [list(range(side, count, 2)) for side in (0, 1)]
    side = lax.axis_index(axis) % 2
    copies = jnp.broadcast_to(x[None], (count // 2,) + x.shape).reshape((count // 2 * x.shape[0],) + x.shape[1:])
    half = lax.all_to_all(copies, axis, 0, 0, tiled=True, axis_index_groups=groups)
    other = lax.ppermute(half, axis, pairs)
    return jnp.where(side == 0, jnp.concatenate([half, other]), jnp.concatenate([other, half]))


def local(surface, wet_blocks, legendre, slot_order, love_gain):
    cycle_count, lon_width = surface.shape
    groups = lax.axis_size("lon")
    lon_total = lon_width * groups
    slot_count = legendre.shape[0]
    slot_total = slot_count * groups
    wet_cells = jnp.repeat(wet_blocks, BLK, axis=1).astype(jnp.float32)
    masked = wet_cells * surface
    lon_start = lax.axis_index("lon") * lon_width
    own_orders = lax.dynamic_slice_in_dim(
        slot_order, lax.axis_index("lon") * slot_count, slot_count
    )
    forward_scale = lon_total ** (-0.5)
    fourier = reduce_scatter(forward_dft(masked, slot_order, lon_start, lon_total) * forward_scale, "lon")
    fourier = fourier.reshape(slot_count, 2, cycle_count)
    coefficient = jnp.einsum("krl,kcr->kcl", legendre, fourier, precision=lax.Precision.HIGH)
    degree_whole = paired_all_gather(paired_reduce_scatter(coefficient, "lat"), "lat")
    degree_count = degree_whole.shape[2]
    degrees = jnp.arange(degree_count, dtype=jnp.int32)
    retained = degrees[None, :] >= own_orders[:, None]
    spectrum = jnp.where(retained[:, None, :], love_gain[None, None, :] * degree_whole, 0.0)
    synthesis = (legendre[:, None, :, :] * spectrum[:, :, None, :]).sum(axis=3)
    summed = inverse_dft(lax.all_gather(synthesis, "lon", axis=0, tiled=True), slot_order, lon_start, lon_width, lon_total)
    loading = summed * (2 * slot_total) ** (-0.5)
    potential = masked - 0.6 * loading
    neighbours = neighbour_sum(potential)
    surface_next = wet_cells * (masked + 0.2 * (neighbours - 4.0 * potential))
    return (surface_next, loading)


def solution(mesh):
    return jax.shard_map(
        local,
        mesh=mesh,
        in_specs=(P("lat", "lon"), P("lat", "lon"), P("lon", "lat", None), P(), P()),
        out_specs=(P("lat", "lon"), P("lat", "lon")),
        check_vma=False,
    )
```

```python
import math

import jax
import jax.numpy as jnp
from jax import lax
from jax.sharding import PartitionSpec as P

BLK = 128


def halo(cells, axis, dim):
    count = lax.axis_size(axis)
    ends = count - 1
    head = lax.slice_in_dim(cells, 0, 1, axis=dim)
    tail = lax.slice_in_dim(cells, cells.shape[dim] - 1, cells.shape[dim], axis=dim)
    before = lax.ppermute(tail, axis, [(i, (i + 1) % count) for i in range(ends)])
    after = lax.ppermute(head, axis, [((i + 1) % count, i) for i in range(ends)])
    return before, after


def neighbour_sum(cells):
    up, down = halo(cells, "lat", 0)
    left, right = halo(cells, "lon", 1)
    rows = jnp.concatenate([up, cells[:-1]], axis=0) + jnp.concatenate([cells[1:], down], axis=0)
    cols = jnp.concatenate([left, cells[:, :-1]], axis=1) + jnp.concatenate([cells[:, 1:], right], axis=1)
    return rows + cols


INNER = 32


def dft_tables(order_count, lon_start, lon_width, lon_total):
    period = lon_total // INNER
    outer = jnp.arange(lon_width // INNER, dtype=jnp.int32)
    residue = jnp.arange(period, dtype=jnp.int32)
    alpha = (residue[:, None] * outer[None, :] % period).astype(jnp.float32) * (2.0 * math.pi / period)
    orders = jnp.arange(order_count, dtype=jnp.int32)
    inner = lon_start + jnp.arange(INNER, dtype=jnp.int32)
    beta = (orders[:, None] * inner[None, :] % lon_total).astype(jnp.float32) * (2.0 * math.pi / lon_total)
    beta = beta.reshape(order_count // period, period, INNER)
    return jnp.stack([jnp.cos(alpha), jnp.sin(alpha)]), jnp.cos(beta), jnp.sin(beta)


def forward_dft(masked, slot_order, lon_start, lon_total):
    cycles, lon_width = masked.shape
    order_count = slot_order.shape[0]
    rotor, cb, sb = dft_tables(order_count, lon_start, lon_width, lon_total)
    blocks = masked.reshape(cycles, lon_width // INNER, INNER)
    partial = jnp.einsum("cua,rab->cubr", rotor, blocks, precision=lax.Precision.HIGHEST)
    gc, gs = partial[0][None], partial[1][None]
    fc = (cb[..., None] * gc - sb[..., None] * gs).sum(axis=2)
    fs = (sb[..., None] * gc + cb[..., None] * gs).sum(axis=2)
    by_order = jnp.stack([fc, fs], axis=2).reshape(order_count, 2 * cycles)
    return jnp.take(by_order, slot_order, axis=0, mode="clip", unique_indices=True)


def inverse_dft(synthesis, slot_order, lon_start, lon_width, lon_total):
    order_count, width = synthesis.shape
    cycles = width // 2
    rotor, cb, sb = dft_tables(order_count, lon_start, lon_width, lon_total)
    slots = jnp.arange(order_count, dtype=jnp.int32)
    slot_of = jnp.where(slot_order[None, :] == slots[:, None], slots[None, :], 0).sum(axis=1)
    by_order = jnp.take(synthesis, slot_of, axis=0, mode="clip", unique_indices=True).reshape(cb.shape[0], cb.shape[1], 2, cycles)
    yc, ys = by_order[:, :, 0, None, :], by_order[:, :, 1, None, :]
    hc = (yc * cb[..., None] + ys * sb[..., None]).sum(axis=0)
    hs = (ys * cb[..., None] - yc * sb[..., None]).sum(axis=0)
    out = jnp.einsum("cua,cubr->rab", rotor, jnp.stack([hc, hs]), precision=lax.Precision.HIGHEST)
    return out.reshape(cycles, lon_width)


def reduce_scatter(x, axis):
    count = lax.axis_size(axis)
    moved = lax.all_to_all(x, axis, 0, 0, tiled=True)
    return moved.reshape((count, x.shape[0] // count) + x.shape[1:]).sum(axis=0)


def all_gather(x, axis):
    count = lax.axis_size(axis)
    copies = jnp.broadcast_to(x[None], (count,) + x.shape).reshape((count * x.shape[0],) + x.shape[1:])
    return lax.all_to_all(copies, axis, 0, 0, tiled=True)


def paired_reduce_scatter(x, axis):
    count = lax.axis_size(axis)
    pairs = [(i, i ^ 1) for i in range(count)]
    groups = [list(range(side, count, 2)) for side in (0, 1)]
    side = lax.axis_index(axis) % 2
    half = x.shape[0] // 2
    kept = lax.dynamic_slice_in_dim(x, side * half, half)
    sent = lax.dynamic_slice_in_dim(x, (1 - side) * half, half)
    summed = kept + lax.ppermute(sent, axis, pairs)
    moved = lax.all_to_all(summed, axis, 0, 0, tiled=True, axis_index_groups=groups)
    return moved.reshape((count // 2, half * 2 // count) + x.shape[1:]).sum(axis=0)


def paired_all_gather(x, axis):
    count = lax.axis_size(axis)
    pairs = [(i, i ^ 1) for i in range(count)]
    groups = [list(range(side, count, 2)) for side in (0, 1)]
    side = lax.axis_index(axis) % 2
    copies = jnp.broadcast_to(x[None], (count // 2,) + x.shape).reshape((count // 2 * x.shape[0],) + x.shape[1:])
    half = lax.all_to_all(copies, axis, 0, 0, tiled=True, axis_index_groups=groups)
    other = lax.ppermute(half, axis, pairs)
    return jnp.where(side == 0, jnp.concatenate([half, other]), jnp.concatenate([other, half]))


def local(surface, wet_blocks, legendre, slot_order, love_gain):
    cycle_count, lon_width = surface.shape
    groups = lax.axis_size("lon")
    lon_total = lon_width * groups
    slot_count = legendre.shape[0]
    slot_total = slot_count * groups
    wet_cells = jnp.repeat(wet_blocks, BLK, axis=1).astype(jnp.float32)
    masked = wet_cells * surface
    lon_start = lax.axis_index("lon") * lon_width
    own_orders = lax.dynamic_slice_in_dim(
        slot_order, lax.axis_index("lon") * slot_count, slot_count
    )
    forward_scale = lon_total ** (-0.5)
    fourier = reduce_scatter(forward_dft(masked, slot_order, lon_start, lon_total) * forward_scale, "lon")
    fourier = fourier.reshape(slot_count, 2, cycle_count)
    coefficient = jnp.einsum("krl,kcr->kcl", legendre, fourier, precision=lax.Precision.HIGH)
    degree_whole = paired_all_gather(paired_reduce_scatter(coefficient, "lat"), "lat")
    degree_count = degree_whole.shape[2]
    degrees = jnp.arange(degree_count, dtype=jnp.int32)
    retained = degrees[None, :] >= own_orders[:, None]
    spectrum = jnp.where(retained[:, None, :], love_gain[None, None, :] * degree_whole, 0.0)
    synthesis = (legendre[:, None, :, :] * spectrum[:, :, None, :]).sum(axis=3)
    summed = inverse_dft(lax.all_gather(synthesis.reshape(slot_count, -1), "lon", axis=0, tiled=True), slot_order, lon_start, lon_width, lon_total)
    loading = summed * (2 * slot_total) ** (-0.5)
    potential = masked - 0.6 * loading
    neighbours = neighbour_sum(potential)
    surface_next = wet_cells * (masked + 0.2 * (neighbours - 4.0 * potential))
    return (surface_next, loading)


def solution(mesh):
    return jax.shard_map(
        local,
        mesh=mesh,
        in_specs=(P("lat", "lon"), P("lat", "lon"), P("lon", "lat", None), P(), P()),
        out_specs=(P("lat", "lon"), P("lat", "lon")),
        check_vma=False,
    )
```

```python
import math

import jax
import jax.numpy as jnp
from jax import lax
from jax.sharding import PartitionSpec as P

BLK = 128


def halo(cells, axis, dim):
    count = lax.axis_size(axis)
    ends = count - 1
    head = lax.slice_in_dim(cells, 0, 1, axis=dim)
    tail = lax.slice_in_dim(cells, cells.shape[dim] - 1, cells.shape[dim], axis=dim)
    before = lax.ppermute(tail, axis, [(i, (i + 1) % count) for i in range(ends)])
    after = lax.ppermute(head, axis, [((i + 1) % count, i) for i in range(ends)])
    return before, after


def neighbour_sum(cells):
    up, down = halo(cells, "lat", 0)
    left, right = halo(cells, "lon", 1)
    rows = jnp.concatenate([up, cells[:-1]], axis=0) + jnp.concatenate([cells[1:], down], axis=0)
    cols = jnp.concatenate([left, cells[:, :-1]], axis=1) + jnp.concatenate([cells[:, 1:], right], axis=1)
    return rows + cols


INNER = 32


def dft_tables(order_count, lon_start, lon_width, lon_total):
    period = lon_total // INNER
    outer = jnp.arange(lon_width // INNER, dtype=jnp.int32)
    residue = jnp.arange(period, dtype=jnp.int32)
    alpha = (residue[:, None] * outer[None, :] % period).astype(jnp.float32) * (2.0 * math.pi / period)
    orders = jnp.arange(order_count, dtype=jnp.int32)
    inner = lon_start + jnp.arange(INNER, dtype=jnp.int32)
    beta = (orders[:, None] * inner[None, :] % lon_total).astype(jnp.float32) * (2.0 * math.pi / lon_total)
    beta = beta.reshape(order_count // period, period, INNER)
    return jnp.stack([jnp.cos(alpha), jnp.sin(alpha)]), jnp.cos(beta), jnp.sin(beta)


def forward_dft(masked, slot_order, lon_start, lon_total):
    cycles, lon_width = masked.shape
    order_count = slot_order.shape[0]
    rotor, cb, sb = dft_tables(order_count, lon_start, lon_width, lon_total)
    blocks = masked.reshape(cycles, lon_width // INNER, INNER)
    partial = jnp.einsum("cua,rab->cubr", rotor, blocks, precision=lax.Precision.HIGHEST)
    gc, gs = partial[0][None], partial[1][None]
    fc = (cb[..., None] * gc - sb[..., None] * gs).sum(axis=2)
    fs = (sb[..., None] * gc + cb[..., None] * gs).sum(axis=2)
    by_order = jnp.stack([fc, fs], axis=2).reshape(order_count, 2 * cycles)
    return jnp.take(by_order, slot_order, axis=0, mode="clip", unique_indices=True)


def inverse_dft(synthesis, slot_order, lon_start, lon_width, lon_total):
    order_count, width = synthesis.shape
    cycles = width // 2
    rotor, cb, sb = dft_tables(order_count, lon_start, lon_width, lon_total)
    slots = jnp.arange(order_count, dtype=jnp.int32)
    slot_of = jnp.where(slot_order[None, :] == slots[:, None], slots[None, :], 0).sum(axis=1)
    by_order = jnp.take(synthesis, slot_of, axis=0, mode="clip", unique_indices=True).reshape(cb.shape[0], cb.shape[1], 2, cycles)
    yc, ys = by_order[:, :, 0, None, :], by_order[:, :, 1, None, :]
    hc = (yc * cb[..., None] + ys * sb[..., None]).sum(axis=0)
    hs = (ys * cb[..., None] - yc * sb[..., None]).sum(axis=0)
    out = jnp.einsum("cua,cubr->rab", rotor, jnp.stack([hc, hs]), precision=lax.Precision.HIGHEST)
    return out.reshape(cycles, lon_width)


def reduce_scatter(x, axis):
    count = lax.axis_size(axis)
    moved = lax.all_to_all(x, axis, 0, 0, tiled=True)
    return moved.reshape((count, x.shape[0] // count) + x.shape[1:]).sum(axis=0)


def all_gather(x, axis):
    count = lax.axis_size(axis)
    copies = jnp.broadcast_to(x[None], (count,) + x.shape).reshape((count * x.shape[0],) + x.shape[1:])
    return lax.all_to_all(copies, axis, 0, 0, tiled=True)


def paired_reduce_scatter(x, axis):
    count = lax.axis_size(axis)
    pairs = [(i, i ^ 1) for i in range(count)]
    groups = [list(range(side, count, 2)) for side in (0, 1)]
    side = lax.axis_index(axis) % 2
    half = x.shape[0] // 2
    kept = lax.dynamic_slice_in_dim(x, side * half, half)
    sent = lax.dynamic_slice_in_dim(x, (1 - side) * half, half)
    summed = kept + lax.ppermute(sent, axis, pairs)
    moved = lax.all_to_all(summed, axis, 0, 0, tiled=True, axis_index_groups=groups)
    return moved.reshape((count // 2, half * 2 // count) + x.shape[1:]).sum(axis=0)


def paired_all_gather(x, axis):
    count = lax.axis_size(axis)
    pairs = [(i, i ^ 1) for i in range(count)]
    groups = [list(range(side, count, 2)) for side in (0, 1)]
    side = lax.axis_index(axis) % 2
    copies = jnp.broadcast_to(x[None], (count // 2,) + x.shape).reshape((count // 2 * x.shape[0],) + x.shape[1:])
    half = lax.all_to_all(copies, axis, 0, 0, tiled=True, axis_index_groups=groups)
    other = lax.ppermute(half, axis, pairs)
    return jnp.where(side == 0, jnp.concatenate([half, other]), jnp.concatenate([other, half]))


def local(surface, wet_blocks, legendre, slot_order, love_gain):
    cycle_count, lon_width = surface.shape
    groups = lax.axis_size("lon")
    lon_total = lon_width * groups
    slot_count = legendre.shape[0]
    slot_total = slot_count * groups
    wet_cells = jnp.repeat(wet_blocks, BLK, axis=1).astype(jnp.float32)
    masked = wet_cells * surface
    lon_start = lax.axis_index("lon") * lon_width
    own_orders = lax.dynamic_slice_in_dim(
        slot_order, lax.axis_index("lon") * slot_count, slot_count
    )
    forward_scale = lon_total ** (-0.5)
    fourier = reduce_scatter(forward_dft(masked, slot_order, lon_start, lon_total) * forward_scale, "lon")
    fourier = fourier.reshape(slot_count, 2, cycle_count)
    coefficient = jnp.einsum("krl,kcr->kcl", legendre, fourier, precision=lax.Precision.HIGH)
    degree_whole = paired_all_gather(paired_reduce_scatter(coefficient, "lat"), "lat")
    degree_count = degree_whole.shape[2]
    degrees = jnp.arange(degree_count, dtype=jnp.int32)
    retained = degrees[None, :] >= own_orders[:, None]
    spectrum = jnp.where(retained[:, None, :], love_gain[None, None, :] * degree_whole, 0.0)
    synthesis = (legendre[:, None, :, :] * spectrum[:, :, None, :]).sum(axis=3)
    summed = inverse_dft(all_gather(synthesis.reshape(slot_count, -1), "lon"), slot_order, lon_start, lon_width, lon_total)
    loading = summed * (2 * slot_total) ** (-0.5)
    potential = masked - 0.6 * loading
    neighbours = neighbour_sum(potential)
    surface_next = wet_cells * (masked + 0.2 * (neighbours - 4.0 * potential))
    return (surface_next, loading)


def solution(mesh):
    return jax.shard_map(
        local,
        mesh=mesh,
        in_specs=(P("lat", "lon"), P("lat", "lon"), P("lon", "lat", None), P(), P()),
        out_specs=(P("lat", "lon"), P("lat", "lon")),
        check_vma=False,
    )
```

```python
import math

import jax
import jax.numpy as jnp
from jax import lax
from jax.sharding import PartitionSpec as P

BLK = 128


def halo(cells, axis, dim):
    count = lax.axis_size(axis)
    ends = count - 1
    head = lax.slice_in_dim(cells, 0, 1, axis=dim)
    tail = lax.slice_in_dim(cells, cells.shape[dim] - 1, cells.shape[dim], axis=dim)
    before = lax.ppermute(tail, axis, [(i, (i + 1) % count) for i in range(ends)])
    after = lax.ppermute(head, axis, [((i + 1) % count, i) for i in range(ends)])
    return before, after


def neighbour_sum(cells):
    up, down = halo(cells, "lat", 0)
    left, right = halo(cells, "lon", 1)
    rows = jnp.concatenate([up, cells[:-1]], axis=0) + jnp.concatenate([cells[1:], down], axis=0)
    cols = jnp.concatenate([left, cells[:, :-1]], axis=1) + jnp.concatenate([cells[:, 1:], right], axis=1)
    return rows + cols


INNER = 32


def dft_tables(order_count, lon_start, lon_width, lon_total):
    period = lon_total // INNER
    outer = jnp.arange(lon_width // INNER, dtype=jnp.int32)
    residue = jnp.arange(period, dtype=jnp.int32)
    alpha = (residue[:, None] * outer[None, :] % period).astype(jnp.float32) * (2.0 * math.pi / period)
    orders = jnp.arange(order_count, dtype=jnp.int32)
    inner = lon_start + jnp.arange(INNER, dtype=jnp.int32)
    beta = (orders[:, None] * inner[None, :] % lon_total).astype(jnp.float32) * (2.0 * math.pi / lon_total)
    beta = beta.reshape(order_count // period, period, INNER)
    return jnp.stack([jnp.cos(alpha), jnp.sin(alpha)]), jnp.cos(beta), jnp.sin(beta)


def forward_dft(masked, slot_order, lon_start, lon_total):
    cycles, lon_width = masked.shape
    order_count = slot_order.shape[0]
    rotor, cb, sb = dft_tables(order_count, lon_start, lon_width, lon_total)
    blocks = masked.reshape(cycles, lon_width // INNER, INNER)
    partial = jnp.einsum("cua,rab->cubr", rotor, blocks, precision=lax.Precision.HIGHEST)
    gc, gs = partial[0][None], partial[1][None]
    fc = (cb[..., None] * gc - sb[..., None] * gs).sum(axis=2)
    fs = (sb[..., None] * gc + cb[..., None] * gs).sum(axis=2)
    by_order = jnp.stack([fc, fs], axis=2).reshape(order_count, 2 * cycles)
    return jnp.take(by_order, slot_order, axis=0, mode="clip", unique_indices=True)


def inverse_dft(synthesis, slot_order, lon_start, lon_width, lon_total):
    order_count, width = synthesis.shape
    cycles = width // 2
    rotor, cb, sb = dft_tables(order_count, lon_start, lon_width, lon_total)
    slots = jnp.arange(order_count, dtype=jnp.int32)
    slot_of = jnp.where(slot_order[None, :] == slots[:, None], slots[None, :], 0).sum(axis=1)
    by_order = jnp.take(synthesis, slot_of, axis=0, mode="clip", unique_indices=True).reshape(cb.shape[0], cb.shape[1], 2, cycles)
    yc, ys = by_order[:, :, 0, None, :], by_order[:, :, 1, None, :]
    hc = (yc * cb[..., None] + ys * sb[..., None]).sum(axis=0)
    hs = (ys * cb[..., None] - yc * sb[..., None]).sum(axis=0)
    out = jnp.einsum("cua,cubr->rab", rotor, jnp.stack([hc, hs]), precision=lax.Precision.HIGHEST)
    return out.reshape(cycles, lon_width)


def reduce_scatter(x, axis):
    count = lax.axis_size(axis)
    moved = lax.all_to_all(x, axis, 0, 0, tiled=True)
    return moved.reshape((count, x.shape[0] // count) + x.shape[1:]).sum(axis=0)


def all_gather(x, axis):
    count = lax.axis_size(axis)
    copies = jnp.broadcast_to(x[None], (count,) + x.shape).reshape((count * x.shape[0],) + x.shape[1:])
    return lax.all_to_all(copies, axis, 0, 0, tiled=True)


def paired_reduce_scatter(x, axis):
    count = lax.axis_size(axis)
    pairs = [(i, i ^ 1) for i in range(count)]
    groups = [list(range(side, count, 2)) for side in (0, 1)]
    side = lax.axis_index(axis) % 2
    half = x.shape[0] // 2
    kept = lax.dynamic_slice_in_dim(x, side * half, half)
    sent = lax.dynamic_slice_in_dim(x, (1 - side) * half, half)
    summed = kept + lax.ppermute(sent, axis, pairs)
    moved = lax.all_to_all(summed, axis, 0, 0, tiled=True, axis_index_groups=groups)
    return moved.reshape((count // 2, half * 2 // count) + x.shape[1:]).sum(axis=0)


def paired_all_gather(x, axis):
    count = lax.axis_size(axis)
    pairs = [(i, i ^ 1) for i in range(count)]
    groups = [list(range(side, count, 2)) for side in (0, 1)]
    side = lax.axis_index(axis) % 2
    copies = jnp.broadcast_to(x[None], (count // 2,) + x.shape).reshape((count // 2 * x.shape[0],) + x.shape[1:])
    half = lax.all_to_all(copies, axis, 0, 0, tiled=True, axis_index_groups=groups)
    other = lax.ppermute(half, axis, pairs)
    return jnp.where(side == 0, jnp.concatenate([half, other]), jnp.concatenate([other, half]))


def local(surface, wet_blocks, legendre, slot_order, love_gain):
    cycle_count, lon_width = surface.shape
    groups = lax.axis_size("lon")
    lon_total = lon_width * groups
    slot_count = legendre.shape[0]
    slot_total = slot_count * groups
    wet_cells = jnp.repeat(wet_blocks, BLK, axis=1).astype(jnp.float32)
    masked = wet_cells * surface
    lon_start = lax.axis_index("lon") * lon_width
    own_orders = lax.dynamic_slice_in_dim(
        slot_order, lax.axis_index("lon") * slot_count, slot_count
    )
    forward_scale = lon_total ** (-0.5)
    fourier = reduce_scatter(forward_dft(masked, slot_order, lon_start, lon_total) * forward_scale, "lon")
    fourier = fourier.reshape(slot_count, 2, cycle_count)
    coefficient = (legendre[:, None, :, :] * fourier[:, :, :, None]).sum(axis=2)
    degree_whole = paired_all_gather(paired_reduce_scatter(coefficient, "lat"), "lat")
    degree_count = degree_whole.shape[2]
    degrees = jnp.arange(degree_count, dtype=jnp.int32)
    retained = degrees[None, :] >= own_orders[:, None]
    spectrum = jnp.where(retained[:, None, :], love_gain[None, None, :] * degree_whole, 0.0)
    synthesis = (legendre[:, None, :, :] * spectrum[:, :, None, :]).sum(axis=3)
    summed = inverse_dft(all_gather(synthesis.reshape(slot_count, -1), "lon"), slot_order, lon_start, lon_width, lon_total)
    loading = summed * (2 * slot_total) ** (-0.5)
    potential = masked - 0.6 * loading
    neighbours = neighbour_sum(potential)
    surface_next = wet_cells * (masked + 0.2 * (neighbours - 4.0 * potential))
    return (surface_next, loading)


def solution(mesh):
    return jax.shard_map(
        local,
        mesh=mesh,
        in_specs=(P("lat", "lon"), P("lat", "lon"), P("lon", "lat", None), P(), P()),
        out_specs=(P("lat", "lon"), P("lat", "lon")),
        check_vma=False,
    )
```

```python
import math

import jax
import jax.numpy as jnp
from jax import lax
from jax.sharding import PartitionSpec as P

BLK = 128


def halo(cells, axis, dim):
    count = lax.axis_size(axis)
    ends = count - 1
    head = lax.slice_in_dim(cells, 0, 1, axis=dim)
    tail = lax.slice_in_dim(cells, cells.shape[dim] - 1, cells.shape[dim], axis=dim)
    before = lax.ppermute(tail, axis, [(i, (i + 1) % count) for i in range(ends)])
    after = lax.ppermute(head, axis, [((i + 1) % count, i) for i in range(ends)])
    return before, after


def neighbour_sum(cells):
    up, down = halo(cells, "lat", 0)
    left, right = halo(cells, "lon", 1)
    rows = jnp.concatenate([up, cells[:-1]], axis=0) + jnp.concatenate([cells[1:], down], axis=0)
    cols = jnp.concatenate([left, cells[:, :-1]], axis=1) + jnp.concatenate([cells[:, 1:], right], axis=1)
    return rows + cols


INNER = 32


def dft_tables(order_count, lon_start, lon_width, lon_total):
    period = lon_total // INNER
    outer = jnp.arange(lon_width // INNER, dtype=jnp.int32)
    residue = jnp.arange(period, dtype=jnp.int32)
    alpha = (residue[:, None] * outer[None, :] % period).astype(jnp.float32) * (2.0 * math.pi / period)
    orders = jnp.arange(order_count, dtype=jnp.int32)
    inner = lon_start + jnp.arange(INNER, dtype=jnp.int32)
    beta = (orders[:, None] * inner[None, :] % lon_total).astype(jnp.float32) * (2.0 * math.pi / lon_total)
    beta = beta.reshape(order_count // period, period, INNER)
    return jnp.stack([jnp.cos(alpha), jnp.sin(alpha)]), jnp.cos(beta), jnp.sin(beta)


def forward_dft(masked, slot_order, lon_start, lon_total):
    cycles, lon_width = masked.shape
    order_count = slot_order.shape[0]
    rotor, cb, sb = dft_tables(order_count, lon_start, lon_width, lon_total)
    blocks = masked.reshape(cycles, lon_width // INNER, INNER)
    partial = jnp.einsum("cua,rab->cubr", rotor, blocks, precision=lax.Precision.HIGHEST)
    gc, gs = partial[0][None], partial[1][None]
    fc = (cb[..., None] * gc - sb[..., None] * gs).sum(axis=2)
    fs = (sb[..., None] * gc + cb[..., None] * gs).sum(axis=2)
    by_order = jnp.stack([fc, fs], axis=2).reshape(order_count, 2 * cycles)
    return jnp.take(by_order, slot_order, axis=0, mode="clip", unique_indices=True)


def inverse_dft(synthesis, slot_order, lon_start, lon_width, lon_total):
    order_count, width = synthesis.shape
    cycles = width // 2
    rotor, cb, sb = dft_tables(order_count, lon_start, lon_width, lon_total)
    slots = jnp.arange(order_count, dtype=jnp.int32)
    slot_of = jnp.where(slot_order[None, :] == slots[:, None], slots[None, :], 0).sum(axis=1)
    by_order = jnp.take(synthesis, slot_of, axis=0, mode="clip", unique_indices=True).reshape(cb.shape[0], cb.shape[1], 2, cycles)
    yc, ys = by_order[:, :, 0, None, :], by_order[:, :, 1, None, :]
    hc = (yc * cb[..., None] + ys * sb[..., None]).sum(axis=0)
    hs = (ys * cb[..., None] - yc * sb[..., None]).sum(axis=0)
    out = jnp.einsum("cua,cubr->rab", rotor, jnp.stack([hc, hs]), precision=lax.Precision.HIGHEST)
    return out.reshape(cycles, lon_width)


def reduce_scatter(x, axis):
    count = lax.axis_size(axis)
    moved = lax.all_to_all(x, axis, 0, 0, tiled=True)
    return moved.reshape((count, x.shape[0] // count) + x.shape[1:]).sum(axis=0)


def all_gather(x, axis):
    count = lax.axis_size(axis)
    copies = jnp.broadcast_to(x[None], (count,) + x.shape).reshape((count * x.shape[0],) + x.shape[1:])
    return lax.all_to_all(copies, axis, 0, 0, tiled=True)


def paired_reduce_scatter(x, axis):
    count = lax.axis_size(axis)
    pairs = [(i, i ^ 1) for i in range(count)]
    groups = [list(range(side, count, 2)) for side in (0, 1)]
    side = lax.axis_index(axis) % 2
    half = x.shape[0] // 2
    kept = lax.dynamic_slice_in_dim(x, side * half, half)
    sent = lax.dynamic_slice_in_dim(x, (1 - side) * half, half)
    summed = kept + lax.ppermute(sent, axis, pairs)
    moved = lax.all_to_all(summed, axis, 0, 0, tiled=True, axis_index_groups=groups)
    return moved.reshape((count // 2, half * 2 // count) + x.shape[1:]).sum(axis=0)


def paired_all_gather(x, axis):
    count = lax.axis_size(axis)
    pairs = [(i, i ^ 1) for i in range(count)]
    groups = [list(range(side, count, 2)) for side in (0, 1)]
    side = lax.axis_index(axis) % 2
    copies = jnp.broadcast_to(x[None], (count // 2,) + x.shape).reshape((count // 2 * x.shape[0],) + x.shape[1:])
    half = lax.all_to_all(copies, axis, 0, 0, tiled=True, axis_index_groups=groups)
    other = lax.ppermute(half, axis, pairs)
    return jnp.where(side == 0, jnp.concatenate([half, other]), jnp.concatenate([other, half]))


def local(surface, wet_blocks, legendre, slot_order, love_gain):
    cycle_count, lon_width = surface.shape
    groups = lax.axis_size("lon")
    lon_total = lon_width * groups
    slot_count = legendre.shape[0]
    slot_total = slot_count * groups
    wet_cells = jnp.repeat(wet_blocks, BLK, axis=1).astype(jnp.float32)
    masked = wet_cells * surface
    lon_start = lax.axis_index("lon") * lon_width
    own_orders = lax.dynamic_slice_in_dim(
        slot_order, lax.axis_index("lon") * slot_count, slot_count
    )
    forward_scale = lon_total ** (-0.5)
    fourier = reduce_scatter(forward_dft(masked, slot_order, lon_start, lon_total) * forward_scale, "lon")
    fourier = fourier.reshape(slot_count, 2, cycle_count)
    coefficient = jnp.einsum("krl,kcr->kcl", legendre, fourier, precision=lax.Precision.HIGH)
    flat = coefficient.reshape(slot_count, -1)
    degree_whole = paired_all_gather(paired_reduce_scatter(flat, "lat"), "lat").reshape(coefficient.shape)
    degree_count = degree_whole.shape[2]
    degrees = jnp.arange(degree_count, dtype=jnp.int32)
    retained = degrees[None, :] >= own_orders[:, None]
    spectrum = jnp.where(retained[:, None, :], love_gain[None, None, :] * degree_whole, 0.0)
    synthesis = (legendre[:, None, :, :] * spectrum[:, :, None, :]).sum(axis=3)
    summed = inverse_dft(all_gather(synthesis.reshape(slot_count, -1), "lon"), slot_order, lon_start, lon_width, lon_total)
    loading = summed * (2 * slot_total) ** (-0.5)
    potential = masked - 0.6 * loading
    neighbours = neighbour_sum(potential)
    surface_next = wet_cells * (masked + 0.2 * (neighbours - 4.0 * potential))
    return (surface_next, loading)


def solution(mesh):
    return jax.shard_map(
        local,
        mesh=mesh,
        in_specs=(P("lat", "lon"), P("lat", "lon"), P("lon", "lat", None), P(), P()),
        out_specs=(P("lat", "lon"), P("lat", "lon")),
        check_vma=False,
    )
```

```python
import math

import jax
import jax.numpy as jnp
from jax import lax
from jax.sharding import PartitionSpec as P

BLK = 128


def halo(cells, axis, dim):
    count = lax.axis_size(axis)
    ends = count - 1
    head = lax.slice_in_dim(cells, 0, 1, axis=dim)
    tail = lax.slice_in_dim(cells, cells.shape[dim] - 1, cells.shape[dim], axis=dim)
    before = lax.ppermute(tail, axis, [(i, (i + 1) % count) for i in range(ends)])
    after = lax.ppermute(head, axis, [((i + 1) % count, i) for i in range(ends)])
    return before, after


def neighbour_sum(cells):
    up, down = halo(cells, "lat", 0)
    left, right = halo(cells, "lon", 1)
    rows = jnp.concatenate([up, cells[:-1]], axis=0) + jnp.concatenate([cells[1:], down], axis=0)
    cols = jnp.concatenate([left, cells[:, :-1]], axis=1) + jnp.concatenate([cells[:, 1:], right], axis=1)
    return rows + cols


INNER = 32


def dft_tables(order_count, lon_start, lon_width, lon_total):
    period = lon_total // INNER
    outer = jnp.arange(lon_width // INNER, dtype=jnp.int32)
    residue = jnp.arange(period, dtype=jnp.int32)
    alpha = (residue[:, None] * outer[None, :] % period).astype(jnp.float32) * (2.0 * math.pi / period)
    orders = jnp.arange(order_count, dtype=jnp.int32)
    inner = lon_start + jnp.arange(INNER, dtype=jnp.int32)
    beta = (orders[:, None] * inner[None, :] % lon_total).astype(jnp.float32) * (2.0 * math.pi / lon_total)
    beta = beta.reshape(order_count // period, period, INNER)
    return jnp.stack([jnp.cos(alpha), jnp.sin(alpha)]), jnp.cos(beta), jnp.sin(beta)


def forward_dft(masked, slot_order, lon_start, lon_total):
    cycles, lon_width = masked.shape
    order_count = slot_order.shape[0]
    rotor, cb, sb = dft_tables(order_count, lon_start, lon_width, lon_total)
    blocks = masked.reshape(cycles, lon_width // INNER, INNER)
    partial = jnp.einsum("cua,rab->cubr", rotor, blocks, precision=lax.Precision.HIGH)
    gc, gs = partial[0][None], partial[1][None]
    fc = (cb[..., None] * gc - sb[..., None] * gs).sum(axis=2)
    fs = (sb[..., None] * gc + cb[..., None] * gs).sum(axis=2)
    by_order = jnp.stack([fc, fs], axis=2).reshape(order_count, 2 * cycles)
    return jnp.take(by_order, slot_order, axis=0, mode="clip", unique_indices=True)


def inverse_dft(synthesis, slot_order, lon_start, lon_width, lon_total):
    order_count, width = synthesis.shape
    cycles = width // 2
    rotor, cb, sb = dft_tables(order_count, lon_start, lon_width, lon_total)
    slots = jnp.arange(order_count, dtype=jnp.int32)
    slot_of = jnp.where(slot_order[None, :] == slots[:, None], slots[None, :], 0).sum(axis=1)
    by_order = jnp.take(synthesis, slot_of, axis=0, mode="clip", unique_indices=True).reshape(cb.shape[0], cb.shape[1], 2, cycles)
    yc, ys = by_order[:, :, 0, None, :], by_order[:, :, 1, None, :]
    hc = (yc * cb[..., None] + ys * sb[..., None]).sum(axis=0)
    hs = (ys * cb[..., None] - yc * sb[..., None]).sum(axis=0)
    out = jnp.einsum("cua,cubr->rab", rotor, jnp.stack([hc, hs]), precision=lax.Precision.HIGH)
    return out.reshape(cycles, lon_width)


def reduce_scatter(x, axis):
    count = lax.axis_size(axis)
    moved = lax.all_to_all(x, axis, 0, 0, tiled=True)
    return moved.reshape((count, x.shape[0] // count) + x.shape[1:]).sum(axis=0)


def all_gather(x, axis):
    count = lax.axis_size(axis)
    copies = jnp.broadcast_to(x[None], (count,) + x.shape).reshape((count * x.shape[0],) + x.shape[1:])
    return lax.all_to_all(copies, axis, 0, 0, tiled=True)


def paired_reduce_scatter(x, axis):
    count = lax.axis_size(axis)
    pairs = [(i, i ^ 1) for i in range(count)]
    groups = [list(range(side, count, 2)) for side in (0, 1)]
    side = lax.axis_index(axis) % 2
    half = x.shape[0] // 2
    kept = lax.dynamic_slice_in_dim(x, side * half, half)
    sent = lax.dynamic_slice_in_dim(x, (1 - side) * half, half)
    summed = kept + lax.ppermute(sent, axis, pairs)
    moved = lax.all_to_all(summed, axis, 0, 0, tiled=True, axis_index_groups=groups)
    return moved.reshape((count // 2, half * 2 // count) + x.shape[1:]).sum(axis=0)


def paired_all_gather(x, axis):
    count = lax.axis_size(axis)
    pairs = [(i, i ^ 1) for i in range(count)]
    groups = [list(range(side, count, 2)) for side in (0, 1)]
    side = lax.axis_index(axis) % 2
    copies = jnp.broadcast_to(x[None], (count // 2,) + x.shape).reshape((count // 2 * x.shape[0],) + x.shape[1:])
    half = lax.all_to_all(copies, axis, 0, 0, tiled=True, axis_index_groups=groups)
    other = lax.ppermute(half, axis, pairs)
    return jnp.where(side == 0, jnp.concatenate([half, other]), jnp.concatenate([other, half]))


def local(surface, wet_blocks, legendre, slot_order, love_gain):
    cycle_count, lon_width = surface.shape
    groups = lax.axis_size("lon")
    lon_total = lon_width * groups
    slot_count = legendre.shape[0]
    slot_total = slot_count * groups
    wet_cells = jnp.repeat(wet_blocks, BLK, axis=1).astype(jnp.float32)
    masked = wet_cells * surface
    lon_start = lax.axis_index("lon") * lon_width
    own_orders = lax.dynamic_slice_in_dim(
        slot_order, lax.axis_index("lon") * slot_count, slot_count
    )
    forward_scale = lon_total ** (-0.5)
    fourier = reduce_scatter(forward_dft(masked, slot_order, lon_start, lon_total) * forward_scale, "lon")
    fourier = fourier.reshape(slot_count, 2, cycle_count)
    coefficient = jnp.einsum("krl,kcr->kcl", legendre, fourier, precision=lax.Precision.HIGH)
    degree_whole = paired_all_gather(paired_reduce_scatter(coefficient, "lat"), "lat")
    degree_count = degree_whole.shape[2]
    degrees = jnp.arange(degree_count, dtype=jnp.int32)
    retained = degrees[None, :] >= own_orders[:, None]
    spectrum = jnp.where(retained[:, None, :], love_gain[None, None, :] * degree_whole, 0.0)
    synthesis = (legendre[:, None, :, :] * spectrum[:, :, None, :]).sum(axis=3)
    summed = inverse_dft(all_gather(synthesis.reshape(slot_count, -1), "lon"), slot_order, lon_start, lon_width, lon_total)
    loading = summed * (2 * slot_total) ** (-0.5)
    potential = masked - 0.6 * loading
    neighbours = neighbour_sum(potential)
    surface_next = wet_cells * (masked + 0.2 * (neighbours - 4.0 * potential))
    return (surface_next, loading)


def solution(mesh):
    return jax.shard_map(
        local,
        mesh=mesh,
        in_specs=(P("lat", "lon"), P("lat", "lon"), P("lon", "lat", None), P(), P()),
        out_specs=(P("lat", "lon"), P("lat", "lon")),
        check_vma=False,
    )
```

```python
import math

import jax
import jax.numpy as jnp
from jax import lax
from jax.sharding import PartitionSpec as P

BLK = 128


def halo(cells, axis, dim):
    count = lax.axis_size(axis)
    ends = count - 1
    head = lax.slice_in_dim(cells, 0, 1, axis=dim)
    tail = lax.slice_in_dim(cells, cells.shape[dim] - 1, cells.shape[dim], axis=dim)
    before = lax.ppermute(tail, axis, [(i, (i + 1) % count) for i in range(ends)])
    after = lax.ppermute(head, axis, [((i + 1) % count, i) for i in range(ends)])
    return before, after


def neighbour_sum(cells):
    up, down = halo(cells, "lat", 0)
    left, right = halo(cells, "lon", 1)
    rows = jnp.concatenate([up, cells[:-1]], axis=0) + jnp.concatenate([cells[1:], down], axis=0)
    cols = jnp.concatenate([left, cells[:, :-1]], axis=1) + jnp.concatenate([cells[:, 1:], right], axis=1)
    return rows + cols


INNER = 32


def dft_tables(order_count, lon_start, lon_width, lon_total):
    period = lon_total // INNER
    outer = jnp.arange(lon_width // INNER, dtype=jnp.int32)
    residue = jnp.arange(period, dtype=jnp.int32)
    alpha = (residue[:, None] * outer[None, :] % period).astype(jnp.float32) * (2.0 * math.pi / period)
    orders = jnp.arange(order_count, dtype=jnp.int32)
    inner = lon_start + jnp.arange(INNER, dtype=jnp.int32)
    beta = (orders[:, None] * inner[None, :] % lon_total).astype(jnp.float32) * (2.0 * math.pi / lon_total)
    beta = beta.reshape(order_count // period, period, INNER)
    return jnp.stack([jnp.cos(alpha), jnp.sin(alpha)]), jnp.cos(beta), jnp.sin(beta)


def forward_dft(masked, slot_order, lon_start, lon_total):
    cycles, lon_width = masked.shape
    order_count = slot_order.shape[0]
    rotor, cb, sb = dft_tables(order_count, lon_start, lon_width, lon_total)
    blocks = masked.reshape(cycles, lon_width // INNER, INNER)
    partial = jnp.einsum("cua,rab->cubr", rotor, blocks, precision=lax.Precision.HIGH)
    gc, gs = partial[0][None], partial[1][None]
    fc = (cb[..., None] * gc - sb[..., None] * gs).sum(axis=2)
    fs = (sb[..., None] * gc + cb[..., None] * gs).sum(axis=2)
    by_order = jnp.stack([fc, fs], axis=2).reshape(order_count, 2 * cycles)
    return jnp.take(by_order, slot_order, axis=0, mode="clip", unique_indices=True)


def inverse_dft(synthesis, slot_order, lon_start, lon_width, lon_total):
    order_count, width = synthesis.shape
    cycles = width // 2
    rotor, cb, sb = dft_tables(order_count, lon_start, lon_width, lon_total)
    slots = jnp.arange(order_count, dtype=jnp.int32)
    slot_of = jnp.where(slot_order[None, :] == slots[:, None], slots[None, :], 0).sum(axis=1)
    by_order = jnp.take(synthesis, slot_of, axis=0, mode="clip", unique_indices=True).reshape(cb.shape[0], cb.shape[1], 2, cycles)
    yc, ys = by_order[:, :, 0, None, :], by_order[:, :, 1, None, :]
    hc = (yc * cb[..., None] + ys * sb[..., None]).sum(axis=0)
    hs = (ys * cb[..., None] - yc * sb[..., None]).sum(axis=0)
    out = jnp.einsum("cua,cubr->rab", rotor, jnp.stack([hc, hs]), precision=lax.Precision.HIGH)
    return out.reshape(cycles, lon_width)


def reduce_scatter(x, axis):
    count = lax.axis_size(axis)
    moved = lax.all_to_all(x, axis, 0, 0, tiled=True)
    return moved.reshape((count, x.shape[0] // count) + x.shape[1:]).sum(axis=0)


def all_gather(x, axis):
    count = lax.axis_size(axis)
    copies = jnp.broadcast_to(x[None], (count,) + x.shape).reshape((count * x.shape[0],) + x.shape[1:])
    return lax.all_to_all(copies, axis, 0, 0, tiled=True)


def paired_reduce_scatter(x, axis):
    count = lax.axis_size(axis)
    pairs = [(i, i ^ 1) for i in range(count)]
    groups = [list(range(side, count, 2)) for side in (0, 1)]
    side = lax.axis_index(axis) % 2
    half = x.shape[0] // 2
    kept = lax.dynamic_slice_in_dim(x, side * half, half)
    sent = lax.dynamic_slice_in_dim(x, (1 - side) * half, half)
    summed = kept + lax.ppermute(sent, axis, pairs)
    moved = lax.all_to_all(summed, axis, 0, 0, tiled=True, axis_index_groups=groups)
    return moved.reshape((count // 2, half * 2 // count) + x.shape[1:]).sum(axis=0)


def paired_all_gather(x, axis):
    count = lax.axis_size(axis)
    groups = [list(range(side, count, 2)) for side in (0, 1)]
    copies = jnp.broadcast_to(x[None], (count // 2,) + x.shape).reshape((count // 2 * x.shape[0],) + x.shape[1:])
    half = lax.all_to_all(copies, axis, 0, 0, tiled=True, axis_index_groups=groups)
    couples = [[i, i + 1] for i in range(0, count, 2)]
    both = jnp.broadcast_to(half[None], (2,) + half.shape).reshape((2 * half.shape[0],) + half.shape[1:])
    return lax.all_to_all(both, axis, 0, 0, tiled=True, axis_index_groups=couples)


def local(surface, wet_blocks, legendre, slot_order, love_gain):
    cycle_count, lon_width = surface.shape
    groups = lax.axis_size("lon")
    lon_total = lon_width * groups
    slot_count = legendre.shape[0]
    slot_total = slot_count * groups
    wet_cells = jnp.repeat(wet_blocks, BLK, axis=1).astype(jnp.float32)
    masked = wet_cells * surface
    lon_start = lax.axis_index("lon") * lon_width
    own_orders = lax.dynamic_slice_in_dim(
        slot_order, lax.axis_index("lon") * slot_count, slot_count
    )
    forward_scale = lon_total ** (-0.5)
    fourier = reduce_scatter(forward_dft(masked, slot_order, lon_start, lon_total) * forward_scale, "lon")
    fourier = fourier.reshape(slot_count, 2, cycle_count)
    coefficient = jnp.einsum("krl,kcr->kcl", legendre, fourier, precision=lax.Precision.HIGH)
    degree_whole = paired_all_gather(paired_reduce_scatter(coefficient, "lat"), "lat")
    degree_count = degree_whole.shape[2]
    degrees = jnp.arange(degree_count, dtype=jnp.int32)
    retained = degrees[None, :] >= own_orders[:, None]
    spectrum = jnp.where(retained[:, None, :], love_gain[None, None, :] * degree_whole, 0.0)
    synthesis = (legendre[:, None, :, :] * spectrum[:, :, None, :]).sum(axis=3)
    summed = inverse_dft(all_gather(synthesis.reshape(slot_count, -1), "lon"), slot_order, lon_start, lon_width, lon_total)
    loading = summed * (2 * slot_total) ** (-0.5)
    potential = masked - 0.6 * loading
    neighbours = neighbour_sum(potential)
    surface_next = wet_cells * (masked + 0.2 * (neighbours - 4.0 * potential))
    return (surface_next, loading)


def solution(mesh):
    return jax.shard_map(
        local,
        mesh=mesh,
        in_specs=(P("lat", "lon"), P("lat", "lon"), P("lon", "lat", None), P(), P()),
        out_specs=(P("lat", "lon"), P("lat", "lon")),
        check_vma=False,
    )
```

```python
import math

import jax
import jax.numpy as jnp
from jax import lax
from jax.sharding import PartitionSpec as P

BLK = 128


def halo(cells, axis, dim):
    count = lax.axis_size(axis)
    ends = count - 1
    head = lax.slice_in_dim(cells, 0, 1, axis=dim)
    tail = lax.slice_in_dim(cells, cells.shape[dim] - 1, cells.shape[dim], axis=dim)
    before = lax.ppermute(tail, axis, [(i, (i + 1) % count) for i in range(ends)])
    after = lax.ppermute(head, axis, [((i + 1) % count, i) for i in range(ends)])
    return before, after


def neighbour_sum(cells):
    up, down = halo(cells, "lat", 0)
    left, right = halo(cells, "lon", 1)
    rows = jnp.concatenate([up, cells[:-1]], axis=0) + jnp.concatenate([cells[1:], down], axis=0)
    cols = jnp.concatenate([left, cells[:, :-1]], axis=1) + jnp.concatenate([cells[:, 1:], right], axis=1)
    return rows + cols


INNER = 32


def dft_tables(order_count, lon_start, lon_width, lon_total):
    period = lon_total // INNER
    outer = jnp.arange(lon_width // INNER, dtype=jnp.int32)
    residue = jnp.arange(period, dtype=jnp.int32)
    alpha = (residue[:, None] * outer[None, :] % period).astype(jnp.float32) * (2.0 * math.pi / period)
    orders = jnp.arange(order_count, dtype=jnp.int32)
    inner = lon_start + jnp.arange(INNER, dtype=jnp.int32)
    beta = (orders[:, None] * inner[None, :] % lon_total).astype(jnp.float32) * (2.0 * math.pi / lon_total)
    beta = beta.reshape(order_count // period, period, INNER)
    return jnp.stack([jnp.cos(alpha), jnp.sin(alpha)]), jnp.cos(beta), jnp.sin(beta)


def forward_dft(masked, slot_order, lon_start, lon_total, scale):
    cycles, lon_width = masked.shape
    order_count = slot_order.shape[0]
    rotor, cb, sb = dft_tables(order_count, lon_start, lon_width, lon_total)
    rotor = rotor * scale
    blocks = masked.reshape(cycles, lon_width // INNER, INNER)
    partial = jnp.einsum("cua,rab->cubr", rotor, blocks, precision=lax.Precision.HIGH)
    gc, gs = partial[0][None], partial[1][None]
    fc = (cb[..., None] * gc - sb[..., None] * gs).sum(axis=2)
    fs = (sb[..., None] * gc + cb[..., None] * gs).sum(axis=2)
    by_order = jnp.stack([fc, fs], axis=2).reshape(order_count, 2 * cycles)
    return jnp.take(by_order, slot_order, axis=0, mode="clip", unique_indices=True)


def inverse_dft(synthesis, slot_order, lon_start, lon_width, lon_total, scale):
    order_count, width = synthesis.shape
    cycles = width // 2
    rotor, cb, sb = dft_tables(order_count, lon_start, lon_width, lon_total)
    rotor = rotor * scale
    slots = jnp.arange(order_count, dtype=jnp.int32)
    slot_of = jnp.where(slot_order[None, :] == slots[:, None], slots[None, :], 0).sum(axis=1)
    by_order = jnp.take(synthesis, slot_of, axis=0, mode="clip", unique_indices=True).reshape(cb.shape[0], cb.shape[1], 2, cycles)
    yc, ys = by_order[:, :, 0, None, :], by_order[:, :, 1, None, :]
    hc = (yc * cb[..., None] + ys * sb[..., None]).sum(axis=0)
    hs = (ys * cb[..., None] - yc * sb[..., None]).sum(axis=0)
    out = jnp.einsum("cua,cubr->rab", rotor, jnp.stack([hc, hs]), precision=lax.Precision.HIGH)
    return out.reshape(cycles, lon_width)


def reduce_scatter(x, axis):
    count = lax.axis_size(axis)
    moved = lax.all_to_all(x, axis, 0, 0, tiled=True)
    return moved.reshape((count, x.shape[0] // count) + x.shape[1:]).sum(axis=0)


def all_gather(x, axis):
    count = lax.axis_size(axis)
    copies = jnp.broadcast_to(x[None], (count,) + x.shape).reshape((count * x.shape[0],) + x.shape[1:])
    return lax.all_to_all(copies, axis, 0, 0, tiled=True)


def paired_reduce_scatter(x, axis):
    count = lax.axis_size(axis)
    pairs = [(i, i ^ 1) for i in range(count)]
    groups = [list(range(side, count, 2)) for side in (0, 1)]
    side = lax.axis_index(axis) % 2
    half = x.shape[0] // 2
    kept = lax.dynamic_slice_in_dim(x, side * half, half)
    sent = lax.dynamic_slice_in_dim(x, (1 - side) * half, half)
    summed = kept + lax.ppermute(sent, axis, pairs)
    moved = lax.all_to_all(summed, axis, 0, 0, tiled=True, axis_index_groups=groups)
    return moved.reshape((count // 2, half * 2 // count) + x.shape[1:]).sum(axis=0)


def paired_all_gather(x, axis):
    count = lax.axis_size(axis)
    pairs = [(i, i ^ 1) for i in range(count)]
    groups = [list(range(side, count, 2)) for side in (0, 1)]
    side = lax.axis_index(axis) % 2
    copies = jnp.broadcast_to(x[None], (count // 2,) + x.shape).reshape((count // 2 * x.shape[0],) + x.shape[1:])
    half = lax.all_to_all(copies, axis, 0, 0, tiled=True, axis_index_groups=groups)
    other = lax.ppermute(half, axis, pairs)
    return jnp.where(side == 0, jnp.concatenate([half, other]), jnp.concatenate([other, half]))


def local(surface, wet_blocks, legendre, slot_order, love_gain):
    cycle_count, lon_width = surface.shape
    groups = lax.axis_size("lon")
    lon_total = lon_width * groups
    slot_count = legendre.shape[0]
    slot_total = slot_count * groups
    wet_cells = jnp.repeat(wet_blocks, BLK, axis=1).astype(jnp.float32)
    masked = wet_cells * surface
    lon_start = lax.axis_index("lon") * lon_width
    own_orders = lax.dynamic_slice_in_dim(
        slot_order, lax.axis_index("lon") * slot_count, slot_count
    )
    forward_scale = lon_total ** (-0.5)
    fourier = reduce_scatter(forward_dft(masked, slot_order, lon_start, lon_total, forward_scale), "lon")
    fourier = fourier.reshape(slot_count, 2, cycle_count)
    coefficient = jnp.einsum("krl,kcr->kcl", legendre, fourier, precision=lax.Precision.HIGH)
    degree_whole = paired_all_gather(paired_reduce_scatter(coefficient, "lat"), "lat")
    degree_count = degree_whole.shape[2]
    degrees = jnp.arange(degree_count, dtype=jnp.int32)
    retained = degrees[None, :] >= own_orders[:, None]
    spectrum = jnp.where(retained[:, None, :], love_gain[None, None, :] * degree_whole, 0.0)
    synthesis = (legendre[:, None, :, :] * spectrum[:, :, None, :]).sum(axis=3)
    summed = inverse_dft(all_gather(synthesis.reshape(slot_count, -1), "lon"), slot_order, lon_start, lon_width, lon_total, (2 * slot_total) ** (-0.5))
    loading = summed
    potential = masked - 0.6 * loading
    neighbours = neighbour_sum(potential)
    surface_next = wet_cells * (masked + 0.2 * (neighbours - 4.0 * potential))
    return (surface_next, loading)


def solution(mesh):
    return jax.shard_map(
        local,
        mesh=mesh,
        in_specs=(P("lat", "lon"), P("lat", "lon"), P("lon", "lat", None), P(), P()),
        out_specs=(P("lat", "lon"), P("lat", "lon")),
        check_vma=False,
    )
```

```python
import math

import jax
import jax.numpy as jnp
from jax import lax
from jax.sharding import PartitionSpec as P

BLK = 128


def halo(cells, axis, dim):
    count = lax.axis_size(axis)
    ends = count - 1
    head = lax.slice_in_dim(cells, 0, 1, axis=dim)
    tail = lax.slice_in_dim(cells, cells.shape[dim] - 1, cells.shape[dim], axis=dim)
    before = lax.ppermute(tail, axis, [(i, (i + 1) % count) for i in range(ends)])
    after = lax.ppermute(head, axis, [((i + 1) % count, i) for i in range(ends)])
    return before, after


def neighbour_sum(cells):
    up, down = halo(cells, "lat", 0)
    left, right = halo(cells, "lon", 1)
    rows = jnp.concatenate([up, cells[:-1]], axis=0) + jnp.concatenate([cells[1:], down], axis=0)
    cols = jnp.concatenate([left, cells[:, :-1]], axis=1) + jnp.concatenate([cells[:, 1:], right], axis=1)
    return rows + cols


INNER = 32


def dft_tables(order_count, lon_start, lon_width, lon_total):
    period = lon_total // INNER
    outer = jnp.arange(lon_width // INNER, dtype=jnp.int32)
    residue = jnp.arange(period, dtype=jnp.int32)
    alpha = (residue[:, None] * outer[None, :] % period).astype(jnp.float32) * (2.0 * math.pi / period)
    orders = jnp.arange(order_count, dtype=jnp.int32)
    inner = lon_start + jnp.arange(INNER, dtype=jnp.int32)
    beta = (orders[:, None] * inner[None, :] % lon_total).astype(jnp.float32) * (2.0 * math.pi / lon_total)
    beta = beta.reshape(order_count // period, period, INNER)
    return jnp.stack([jnp.cos(alpha), jnp.sin(alpha)]), jnp.cos(beta), jnp.sin(beta)


def forward_dft(masked, slot_order, lon_start, lon_total, scale):
    cycles, lon_width = masked.shape
    order_count = slot_order.shape[0]
    rotor, cb, sb = dft_tables(order_count, lon_start, lon_width, lon_total)
    rotor = rotor * scale
    blocks = masked.reshape(cycles, lon_width // INNER, INNER)
    partial = jnp.einsum("cua,rab->cubr", rotor, blocks, precision=lax.Precision.HIGH)
    gc, gs = partial[0][None], partial[1][None]
    fc = (cb[..., None] * gc - sb[..., None] * gs).sum(axis=2)
    fs = (sb[..., None] * gc + cb[..., None] * gs).sum(axis=2)
    by_order = jnp.stack([fc, fs], axis=2).reshape(order_count, 2 * cycles)
    return jnp.take(by_order, slot_order, axis=0, mode="clip", unique_indices=True)


def inverse_dft(synthesis, slot_order, lon_start, lon_width, lon_total, scale):
    order_count, width = synthesis.shape
    cycles = width // 2
    rotor, cb, sb = dft_tables(order_count, lon_start, lon_width, lon_total)
    rotor = rotor * scale
    slots = jnp.arange(order_count, dtype=jnp.int32)
    slot_of = jnp.where(slot_order[None, :] == slots[:, None], slots[None, :], 0).sum(axis=1)
    by_order = jnp.take(synthesis, slot_of, axis=0, mode="clip", unique_indices=True).reshape(cb.shape[0], cb.shape[1], 2, cycles)
    yc, ys = by_order[:, :, 0, None, :], by_order[:, :, 1, None, :]
    hc = (yc * cb[..., None] + ys * sb[..., None]).sum(axis=0)
    hs = (ys * cb[..., None] - yc * sb[..., None]).sum(axis=0)
    out = jnp.einsum("cua,cubr->rab", rotor, jnp.stack([hc, hs]), precision=lax.Precision.HIGH)
    return out.reshape(cycles, lon_width)


def reduce_scatter(x, axis):
    count = lax.axis_size(axis)
    moved = lax.all_to_all(x, axis, 0, 0, tiled=True)
    return moved.reshape((count, x.shape[0] // count) + x.shape[1:]).sum(axis=0)


def all_gather(x, axis):
    count = lax.axis_size(axis)
    copies = jnp.broadcast_to(x[None], (count,) + x.shape).reshape((count * x.shape[0],) + x.shape[1:])
    return lax.all_to_all(copies, axis, 0, 0, tiled=True)


def paired_reduce_scatter(x, axis):
    count = lax.axis_size(axis)
    pairs = [(i, i ^ 1) for i in range(count)]
    groups = [list(range(side, count, 2)) for side in (0, 1)]
    side = lax.axis_index(axis) % 2
    half = x.shape[0] // 2
    kept = lax.dynamic_slice_in_dim(x, side * half, half)
    sent = lax.dynamic_slice_in_dim(x, (1 - side) * half, half)
    summed = kept + lax.ppermute(sent, axis, pairs)
    moved = lax.all_to_all(summed, axis, 0, 0, tiled=True, axis_index_groups=groups)
    return moved.reshape((count // 2, half * 2 // count) + x.shape[1:]).sum(axis=0)


def paired_all_gather(x, axis):
    count = lax.axis_size(axis)
    pairs = [(i, i ^ 1) for i in range(count)]
    groups = [list(range(side, count, 2)) for side in (0, 1)]
    side = lax.axis_index(axis) % 2
    copies = jnp.broadcast_to(x[None], (count // 2,) + x.shape).reshape((count // 2 * x.shape[0],) + x.shape[1:])
    half = lax.all_to_all(copies, axis, 0, 0, tiled=True, axis_index_groups=groups)
    other = lax.ppermute(half, axis, pairs)
    mine_first = (jnp.arange(2) == side)[:, None, None, None]
    joined = jnp.where(mine_first, half[None], other[None])
    return joined.reshape((2 * half.shape[0],) + half.shape[1:])


def local(surface, wet_blocks, legendre, slot_order, love_gain):
    cycle_count, lon_width = surface.shape
    groups = lax.axis_size("lon")
    lon_total = lon_width * groups
    slot_count = legendre.shape[0]
    slot_total = slot_count * groups
    wet_cells = jnp.repeat(wet_blocks, BLK, axis=1).astype(jnp.float32)
    masked = wet_cells * surface
    lon_start = lax.axis_index("lon") * lon_width
    own_orders = lax.dynamic_slice_in_dim(
        slot_order, lax.axis_index("lon") * slot_count, slot_count
    )
    forward_scale = lon_total ** (-0.5)
    fourier = reduce_scatter(forward_dft(masked, slot_order, lon_start, lon_total, forward_scale), "lon")
    fourier = fourier.reshape(slot_count, 2, cycle_count)
    coefficient = jnp.einsum("krl,kcr->kcl", legendre, fourier, precision=lax.Precision.HIGH)
    degree_whole = paired_all_gather(paired_reduce_scatter(coefficient, "lat"), "lat")
    degree_count = degree_whole.shape[2]
    degrees = jnp.arange(degree_count, dtype=jnp.int32)
    retained = degrees[None, :] >= own_orders[:, None]
    spectrum = jnp.where(retained[:, None, :], love_gain[None, None, :] * degree_whole, 0.0)
    synthesis = (legendre[:, None, :, :] * spectrum[:, :, None, :]).sum(axis=3)
    summed = inverse_dft(all_gather(synthesis.reshape(slot_count, -1), "lon"), slot_order, lon_start, lon_width, lon_total, (2 * slot_total) ** (-0.5))
    loading = summed
    potential = masked - 0.6 * loading
    neighbours = neighbour_sum(potential)
    surface_next = wet_cells * (masked + 0.2 * (neighbours - 4.0 * potential))
    return (surface_next, loading)


def solution(mesh):
    return jax.shard_map(
        local,
        mesh=mesh,
        in_specs=(P("lat", "lon"), P("lat", "lon"), P("lon", "lat", None), P(), P()),
        out_specs=(P("lat", "lon"), P("lat", "lon")),
        check_vma=False,
    )
```
